32 devices in a mesh: store: 8 (over z, y), tp: 4 (over x, core).
Axes of the slice: x: 2, y: 2, z: 4, core: 2. Of those that a mesh axis runs over, the one named last changes fastest.
Arguments:
- query_embeds: bfloat16 [16, 16, 4096], P('store', None, 'tp'), may hold values from -6 to 6
- passage_embeds: bfloat16 [16, 32, 4096], P('store', None, 'tp'), may hold values from -6 to 6
- passage_lengths: int32 [16], P('store'), may hold values from 1 to 32, as said below
- cand_passage: int32 [192], P('store'), may hold values from 0 to 15, as said below
- norm_gain: bfloat16 [4096], replicated, may hold values from 0.099609375 to 1.8984375
- w_qkv: bfloat16 [4096, 16, 384], P(None, 'tp'), may hold values from -1 to 1
Outputs:
- query_attn: bfloat16 [16, 16, 2048], P('store', None, 'tp')
- passage_attn: bfloat16 [192, 32, 2048], P('store', None, 'tp')
The draws below stay inside these ranges and needn't reach their ends.
Inputs may be any that keep to these rules, and one draw needn't show every extreme that they name: `cand_passage`: passage id p is held by store index p // 2 at position p % 2. Among the 24 pairs of one store index, the passages come from as many different store indices as possible, and no store index holds the passages of more than 3 of them. `passage_lengths`: some passage has 32 tokens.
All inputs are finite; a program needn't handle non-finite values.
Results may differ from the reference program's by a relative error of at most 0.023.
The reference program's roundings to bfloat16 on the way count: a program that leaves them out, or rounds other values in their place, can miss the bound.
Values may be sent and summed in bfloat16 or wider, within the bound.
No kernel may reach another device: no remote copies, remote signals or barrier semaphores. Data moves between devices by JAX's collectives and lax.ppermute only.
A program may use at most 128 MiB of HBM per device.

```python
import math
import jax
import jax.numpy as jnp
from jax import lax

D = 4096
HEADS = 16
HD = 128
QLEN = 16
PLEN = 32
CANDS = 12
PASS_DEV = 2
QUERIES = 16
PAIRS_DEV = 24
PAIRS = 192
PASSAGES = 16


def draw_passage_lengths(key, part):
    first_key, second_key = jax.random.split(jax.random.fold_in(key, 11))
    lengths = jax.random.randint(first_key, (PASSAGES,), 1, PLEN + 1)
    marked = jax.random.randint(second_key, (), 0, PASSAGES)
    return jnp.where(jnp.arange(PASSAGES) == marked, PLEN, lengths).astype(jnp.int32)


def draw_cand_passage(key, part):
    first_key, second_key = jax.random.split(jax.random.fold_in(key, 23))
    groups = PAIRS // PAIRS_DEV
    shards = PASSAGES // PASS_DEV
    group_keys = jax.random.split(first_key, groups)
    orders = jax.vmap(lambda one_key: jax.random.permutation(one_key, shards))(group_keys)
    holders = orders[:, jnp.arange(PAIRS_DEV) % shards]
    positions = jax.random.randint(second_key, (groups, PAIRS_DEV), 0, PASS_DEV)
    return (holders * PASS_DEV + positions).reshape(PAIRS).astype(jnp.int32)


def draw_w_qkv(key, part):
    base = jax.random.normal(jax.random.fold_in(key, 37), (D, HEADS, 3 * HD), jnp.float32)
    base = jnp.clip(base, -6.0, 6.0) * D ** (-0.5)
    return jnp.clip(base, -1.0, 1.0).astype(jnp.bfloat16)


def shard_levels(stream_key, dims, cuts, smallest, top_value):
    gain = 1.0
    for axis_at, shards_of in cuts:
        heights = jax.random.uniform(jax.random.fold_in(jax.random.fold_in(stream_key, 6), axis_at), (shards_of,), jnp.float32, smallest / len(cuts), top_value / len(cuts))
        gain = gain * jnp.repeat(jnp.exp(heights), dims[axis_at] // shards_of).reshape((-1,) + (1,) * (len(dims) - 1 - axis_at))
    return gain


def noise(key, dims, scale, most, pieces=(), held_as=jnp.bfloat16):
    result = scale * jax.random.normal(key, dims, jnp.float32)
    if pieces:
        result = result * shard_levels(key, dims, pieces, -0.22, 0.18)
    return jnp.clip(result, -most, most).astype(held_as)


def setup_inputs(seed: int = 0) -> dict:
    keys = jax.random.split(jax.random.key(seed), 7)
    return {
        "query_embeds": noise(keys[0], (QUERIES, QLEN, D), 1.0, 6.0, ((0, 8), (2, 4))),
        "passage_embeds": noise(keys[1], (PASSAGES, PLEN, D), 1.0, 6.0, ((0, 8), (2, 4))),
        "passage_lengths": draw_passage_lengths(jax.random.fold_in(keys[6], 71), 0),
        "cand_passage": draw_cand_passage(jax.random.fold_in(keys[6], 71), 0),
        "norm_gain": jnp.clip(1.0 + 0.18 * jax.random.normal(keys[4], (D,), jnp.float32), 0.099609375, 1.8984375).astype(jnp.bfloat16),
        "w_qkv": draw_w_qkv(jax.random.fold_in(keys[6], 71), 0),
    }


def rms_rows(rows, norm_gain):
    values = rows.astype(jnp.float32)
    meansq = lax.optimization_barrier(jnp.mean(values * values, axis=-1, keepdims=True))
    scaled = values * lax.rsqrt(meansq + 1e-05) * norm_gain.astype(jnp.float32)
    return scaled.astype(jnp.bfloat16)

def rotate_parts(raw, positions, head_dim):
    half_dim = head_dim // 2
    inverse = jnp.exp(jnp.arange(half_dim, dtype=jnp.float32) * (-2.0 * math.log(10000.0) / head_dim))
    angles = positions[:, None] * inverse[None, :]
    cosine = jnp.cos(angles)[:, None, :]
    sine_part = jnp.sin(angles)[:, None, :]

    def turned(block):
        first = block[..., :half_dim]
        second = block[..., half_dim:]
        return jnp.concatenate([first * cosine - second * sine_part, second * cosine + first * sine_part], axis=-1)
    queries = turned(raw[..., :head_dim])
    keyset = turned(raw[..., head_dim:2 * head_dim])
    values = raw[..., 2 * head_dim:]
    return jnp.concatenate([queries, keyset, values], axis=-1).astype(jnp.bfloat16)

def project(rows, positions, norm_gain, weights_flat, heads, head_dim):
    normed = rms_rows(rows, norm_gain)
    raw = jnp.dot(normed, weights_flat, preferred_element_type=jnp.float32)
    raw = raw.reshape(rows.shape[0], heads, 3 * head_dim)
    return rotate_parts(raw, positions, head_dim)

def softmax_rounded(scores, allowed):
    masked = jnp.where(allowed, scores, jnp.float32(-1e+30))
    peak = lax.optimization_barrier(jnp.max(masked, axis=-1, keepdims=True))
    expon = jnp.where(allowed, jnp.exp(masked - peak), jnp.float32(0.0))
    return (expon / lax.optimization_barrier(jnp.sum(expon, axis=-1, keepdims=True))).astype(jnp.bfloat16)

def attend_queries(query_qkv, head_dim):
    count, query_len, heads = (query_qkv.shape[0], query_qkv.shape[1], query_qkv.shape[2])
    scale = head_dim ** (-0.5)
    qparts = query_qkv[..., :head_dim].astype(jnp.float32)
    kparts = query_qkv[..., head_dim:2 * head_dim].astype(jnp.float32)
    vparts = query_qkv[..., 2 * head_dim:].astype(jnp.float32)
    scores = jnp.einsum('bqhd,bkhd->bhqk', qparts, kparts) * scale
    steps_row = jnp.arange(query_len, dtype=jnp.int32)
    allowed = steps_row[:, None] >= steps_row[None, :]
    weights = softmax_rounded(scores, allowed[None, None])
    output = jnp.einsum('bhqk,bkhd->bqhd', weights.astype(jnp.float32), vparts)
    return output.reshape(count, query_len, heads * head_dim).astype(jnp.bfloat16)

def attend_pairs(query_qkv, pair_qkv, pair_lengths, head_dim, cands):
    query_len = query_qkv.shape[1]
    pairs, passage_len, heads = (pair_qkv.shape[0], pair_qkv.shape[1], pair_qkv.shape[2])
    scale = head_dim ** (-0.5)
    repeated = jnp.repeat(query_qkv, cands, axis=0)
    keyset = jnp.concatenate([repeated[..., head_dim:2 * head_dim], pair_qkv[..., head_dim:2 * head_dim]], axis=1)
    values = jnp.concatenate([repeated[..., 2 * head_dim:], pair_qkv[..., 2 * head_dim:]], axis=1)
    scores = jnp.einsum('bihd,bthd->bhit', pair_qkv[..., :head_dim].astype(jnp.float32), keyset.astype(jnp.float32)) * scale
    column = jnp.arange(query_len + passage_len, dtype=jnp.int32) - query_len
    row_index = jnp.arange(passage_len, dtype=jnp.int32)
    allowed = (column[None, None, :] < 0) | (column[None, None, :] <= row_index[None, :, None]) & (column[None, None, :] < pair_lengths[:, None, None])
    weights = softmax_rounded(scores, allowed[:, None])
    output = jnp.einsum('bhit,bthd->bihd', weights.astype(jnp.float32), values.astype(jnp.float32))
    live = row_index[None, :] < pair_lengths[:, None]
    output = jnp.where(live[:, :, None, None], output, jnp.float32(0.0))
    return output.reshape(pairs, passage_len, heads * head_dim).astype(jnp.bfloat16)

def reference(query_embeds, passage_embeds, passage_lengths, cand_passage, norm_gain, w_qkv):
    weights_flat = w_qkv.reshape(D, HEADS * 3 * HD)
    query_rows = query_embeds.reshape(QUERIES * QLEN, D)
    query_pos = jnp.tile(jnp.arange(QLEN, dtype=jnp.float32), QUERIES)
    query_qkv = project(query_rows, query_pos, norm_gain, weights_flat, HEADS, HD).reshape(QUERIES, QLEN, HEADS, 3 * HD)
    passage_rows = passage_embeds.reshape(PASSAGES * PLEN, D)
    passage_pos = QLEN + jnp.tile(jnp.arange(PLEN, dtype=jnp.float32), PASSAGES)
    passage_qkv = project(passage_rows, passage_pos, norm_gain, weights_flat, HEADS, HD).reshape(PASSAGES, PLEN, HEADS, 3 * HD)
    query_attn = attend_queries(query_qkv, HD)

    def one_query(inputs):
        own_qkv, chosen = inputs
        return attend_pairs(own_qkv[None], passage_qkv[chosen], passage_lengths[chosen], HD, CANDS)
    per_query = lax.map(one_query, (query_qkv, cand_passage.reshape(QUERIES, CANDS)))
    passage_attn = per_query.reshape(PAIRS, PLEN, HEADS * HD)
    return (query_attn, passage_attn)
```

```python
import math

import jax
import jax.numpy as jnp
from jax import lax
from jax.sharding import PartitionSpec as P


def rms_rows(rows, norm_gain):
    values = rows.astype(jnp.float32)
    meansq = jnp.mean(values * values, axis=-1, keepdims=True)
    scaled = values * lax.rsqrt(meansq + 1e-05) * norm_gain.astype(jnp.float32)
    return scaled.astype(jnp.bfloat16)


def rotate_parts(raw, positions, head_dim):
    half_dim = head_dim // 2
    inverse = jnp.exp(
        jnp.arange(half_dim, dtype=jnp.float32) * (-2.0 * math.log(10000.0) / head_dim)
    )
    angles = positions[:, None] * inverse[None, :]
    cosine = jnp.cos(angles)[:, None, :]
    sine_part = jnp.sin(angles)[:, None, :]

    def turned(block):
        first = block[..., :half_dim]
        second = block[..., half_dim:]
        return jnp.concatenate(
            [first * cosine - second * sine_part, second * cosine + first * sine_part], axis=-1
        )

    queries = turned(raw[..., :head_dim])
    keyset = turned(raw[..., head_dim : 2 * head_dim])
    values = raw[..., 2 * head_dim :]
    return jnp.concatenate([queries, keyset, values], axis=-1).astype(jnp.bfloat16)


def softmax_rounded(scores, allowed):
    masked = jnp.where(allowed, scores, jnp.float32(-1e30))
    peak = jnp.max(masked, axis=-1, keepdims=True)
    expon = jnp.where(allowed, jnp.exp(masked - peak), jnp.float32(0.0))
    return (expon / jnp.sum(expon, axis=-1, keepdims=True)).astype(jnp.bfloat16)


def attend_queries(query_qkv, head_dim):
    count, query_len, heads = (query_qkv.shape[0], query_qkv.shape[1], query_qkv.shape[2])
    scale = head_dim ** (-0.5)
    scores = (
        jnp.einsum(
            "bqhd,bkhd->bhqk",
            query_qkv[..., :head_dim],
            query_qkv[..., head_dim : 2 * head_dim],
            preferred_element_type=jnp.float32,
        )
        * scale
    )
    steps_row = jnp.arange(query_len, dtype=jnp.int32)
    allowed = steps_row[:, None] >= steps_row[None, :]
    weights = softmax_rounded(scores, allowed[None, None])
    output = jnp.einsum(
        "bhqk,bkhd->bqhd",
        weights,
        query_qkv[..., 2 * head_dim :],
        preferred_element_type=jnp.float32,
    )
    return output.reshape(count, query_len, heads * head_dim).astype(jnp.bfloat16)


def attend_core(query_kv, pair_qkv, pair_lengths, head_dim):
    query_len = query_kv.shape[1]
    pairs, passage_len, heads = (pair_qkv.shape[0], pair_qkv.shape[1], pair_qkv.shape[2])
    scale = head_dim ** (-0.5)
    keyset = jnp.concatenate(
        [query_kv[..., :head_dim], pair_qkv[..., head_dim : 2 * head_dim]], axis=1
    )
    values = jnp.concatenate([query_kv[..., head_dim:], pair_qkv[..., 2 * head_dim :]], axis=1)
    scores = (
        jnp.einsum(
            "bihd,bthd->bhit", pair_qkv[..., :head_dim], keyset, preferred_element_type=jnp.float32
        )
        * scale
    )
    column = jnp.arange(query_len + passage_len, dtype=jnp.int32) - query_len
    row_index = jnp.arange(passage_len, dtype=jnp.int32)
    allowed = (column[None, None, :] < 0) | (column[None, None, :] <= row_index[None, :, None]) & (
        column[None, None, :] < pair_lengths[:, None, None]
    )
    weights = softmax_rounded(scores, allowed[:, None])
    output = jnp.einsum("bhit,bthd->bihd", weights, values, preferred_element_type=jnp.float32)
    live = row_index[None, :] < pair_lengths[:, None]
    output = jnp.where(live[:, :, None, None], output, jnp.float32(0.0))
    return output.reshape(pairs, passage_len, heads * head_dim).astype(jnp.bfloat16)


def attend_pairs(query_qkv, pair_qkv, pair_lengths, head_dim, cands):
    repeated = jnp.repeat(query_qkv[..., head_dim:], cands, axis=0)
    return attend_core(repeated, pair_qkv, pair_lengths, head_dim)


def local(query_embeds, passage_embeds, passage_lengths, cand_passage, norm_gain, w_qkv):
    quer_count, query_len, width_part = query_embeds.shape
    pass_count, passage_len = (passage_embeds.shape[0], passage_embeds.shape[1])
    pairs_dev = cand_passage.shape[0]
    cands = pairs_dev // quer_count
    heads_part = w_qkv.shape[1]
    head_dim = w_qkv.shape[2] // 3
    weights_flat = w_qkv.reshape(w_qkv.shape[0], heads_part * 3 * head_dim)
    query_rows = query_embeds.reshape(quer_count * query_len, width_part)
    passage_rows = passage_embeds.reshape(pass_count * passage_len, width_part)
    query_pos = jnp.tile(jnp.arange(query_len, dtype=jnp.float32), quer_count)
    passage_pos = query_len + jnp.tile(jnp.arange(passage_len, dtype=jnp.float32), pass_count)
    query_total = quer_count * query_len
    all_rows = jnp.concatenate([query_rows, passage_rows], axis=0)
    full_rows = lax.all_gather(all_rows, "tp", axis=1, tiled=True)
    normed = rms_rows(full_rows, norm_gain)
    raw = jnp.dot(normed, weights_flat, preferred_element_type=jnp.float32)
    raw = raw.reshape(all_rows.shape[0], heads_part, 3 * head_dim)
    projected = rotate_parts(raw, jnp.concatenate([query_pos, passage_pos], axis=0), head_dim)
    query_qkv = projected[:query_total].reshape(quer_count, query_len, heads_part, 3 * head_dim)
    own_qkv = projected[query_total:].reshape(pass_count, passage_len, heads_part, 3 * head_dim)
    store_qkv = lax.all_gather(own_qkv, "store", axis=0, tiled=True)
    store_len = lax.all_gather(passage_lengths, "store", axis=0, tiled=True)
    pair_qkv = store_qkv[cand_passage]
    pair_lengths = store_len[cand_passage]
    query_attn = attend_queries(query_qkv, head_dim)
    passage_attn = attend_pairs(query_qkv, pair_qkv, pair_lengths, head_dim, cands)
    return (query_attn, passage_attn)


def solution(mesh):
    in_specs = (
        P("store", None, "tp"),
        P("store", None, "tp"),
        P("store"),
        P("store"),
        P(),
        P(None, "tp", None),
    )
    out_specs = (P("store", None, "tp"), P("store", None, "tp"))
    return jax.shard_map(local, mesh=mesh, in_specs=in_specs, out_specs=out_specs, check_vma=False)
```

```python
import math

import jax
import jax.numpy as jnp
from jax import lax
from jax.sharding import PartitionSpec as P


def rms_rows(rows, norm_gain):
    values = rows.astype(jnp.float32)
    meansq = jnp.mean(values * values, axis=-1, keepdims=True)
    scaled = values * lax.rsqrt(meansq + 1e-05) * norm_gain.astype(jnp.float32)
    return scaled.astype(jnp.bfloat16)


def rotate_parts(raw, positions, head_dim):
    half_dim = head_dim // 2
    inverse = jnp.exp(
        jnp.arange(half_dim, dtype=jnp.float32) * (-2.0 * math.log(10000.0) / head_dim)
    )
    angles = positions[:, None] * inverse[None, :]
    cosine = jnp.cos(angles)[:, None, :]
    sine_part = jnp.sin(angles)[:, None, :]

    def turned(block):
        first = block[..., :half_dim]
        second = block[..., half_dim:]
        return jnp.concatenate(
            [first * cosine - second * sine_part, second * cosine + first * sine_part], axis=-1
        )

    queries = turned(raw[..., :head_dim])
    keyset = turned(raw[..., head_dim : 2 * head_dim])
    values = raw[..., 2 * head_dim :]
    return jnp.concatenate([queries, keyset, values], axis=-1).astype(jnp.bfloat16)


def softmax_rounded(scores, allowed):
    masked = jnp.where(allowed, scores, jnp.float32(-1e30))
    peak = jnp.max(masked, axis=-1, keepdims=True)
    expon = jnp.where(allowed, jnp.exp(masked - peak), jnp.float32(0.0))
    return (expon / jnp.sum(expon, axis=-1, keepdims=True)).astype(jnp.bfloat16)


def attend_queries(query_qkv, head_dim):
    count, query_len, heads = (query_qkv.shape[0], query_qkv.shape[1], query_qkv.shape[2])
    scale = head_dim ** (-0.5)
    scores = (
        jnp.einsum(
            "bqhd,bkhd->bhqk",
            query_qkv[..., :head_dim],
            query_qkv[..., head_dim : 2 * head_dim],
            preferred_element_type=jnp.float32,
        )
        * scale
    )
    steps_row = jnp.arange(query_len, dtype=jnp.int32)
    allowed = steps_row[:, None] >= steps_row[None, :]
    weights = softmax_rounded(scores, allowed[None, None])
    output = jnp.einsum(
        "bhqk,bkhd->bqhd",
        weights,
        query_qkv[..., 2 * head_dim :],
        preferred_element_type=jnp.float32,
    )
    return output.reshape(count, query_len, heads * head_dim).astype(jnp.bfloat16)


def attend_core(query_kv, pair_qkv, pair_lengths, head_dim):
    query_len = query_kv.shape[1]
    pairs, passage_len, heads = (pair_qkv.shape[0], pair_qkv.shape[1], pair_qkv.shape[2])
    scale = head_dim ** (-0.5)
    keyset = jnp.concatenate(
        [query_kv[..., :head_dim], pair_qkv[..., head_dim : 2 * head_dim]], axis=1
    )
    values = jnp.concatenate([query_kv[..., head_dim:], pair_qkv[..., 2 * head_dim :]], axis=1)
    scores = (
        jnp.einsum(
            "bihd,bthd->bhit", pair_qkv[..., :head_dim], keyset, preferred_element_type=jnp.float32
        )
        * scale
    )
    column = jnp.arange(query_len + passage_len, dtype=jnp.int32) - query_len
    row_index = jnp.arange(passage_len, dtype=jnp.int32)
    allowed = (column[None, None, :] < 0) | (column[None, None, :] <= row_index[None, :, None]) & (
        column[None, None, :] < pair_lengths[:, None, None]
    )
    weights = softmax_rounded(scores, allowed[:, None])
    output = jnp.einsum("bhit,bthd->bihd", weights, values, preferred_element_type=jnp.float32)
    live = row_index[None, :] < pair_lengths[:, None]
    output = jnp.where(live[:, :, None, None], output, jnp.float32(0.0))
    return output.reshape(pairs, passage_len, heads * head_dim).astype(jnp.bfloat16)


def attend_pairs(query_qkv, pair_qkv, pair_lengths, head_dim, cands):
    repeated = jnp.repeat(query_qkv[..., head_dim:], cands, axis=0)
    return attend_core(repeated, pair_qkv, pair_lengths, head_dim)


def local(query_embeds, passage_embeds, passage_lengths, cand_passage, norm_gain, w_qkv):
    quer_count, query_len, width_part = query_embeds.shape
    pass_count, passage_len = (passage_embeds.shape[0], passage_embeds.shape[1])
    pairs_dev = cand_passage.shape[0]
    cands = pairs_dev // quer_count
    heads_part = w_qkv.shape[1]
    head_dim = w_qkv.shape[2] // 3
    query_rows = query_embeds.reshape(quer_count * query_len, width_part)
    passage_rows = passage_embeds.reshape(pass_count * passage_len, width_part)
    query_pos = jnp.tile(jnp.arange(query_len, dtype=jnp.float32), quer_count)
    passage_pos = query_len + jnp.tile(jnp.arange(passage_len, dtype=jnp.float32), pass_count)
    query_total = quer_count * query_len
    all_rows = jnp.concatenate([query_rows, passage_rows], axis=0)
    full_rows = lax.all_gather(all_rows, "tp", axis=1, tiled=True)
    normed = rms_rows(full_rows, norm_gain)
    raw = jnp.einsum("nk,khc->nhc", normed, w_qkv, preferred_element_type=jnp.float32)
    projected = rotate_parts(raw, jnp.concatenate([query_pos, passage_pos], axis=0), head_dim)
    query_qkv = projected[:query_total].reshape(quer_count, query_len, heads_part, 3 * head_dim)
    own_qkv = projected[query_total:].reshape(pass_count, passage_len, heads_part, 3 * head_dim)
    padded = jnp.arange(passage_len, dtype=jnp.int32)[None, :] >= passage_lengths[:, None]
    marker = own_qkv[:, :, 0, head_dim]
    own_qkv = own_qkv.at[:, :, 0, head_dim].set(jnp.where(padded, jnp.inf, marker).astype(own_qkv.dtype))
    store_qkv = lax.all_gather(own_qkv, "store", axis=0, tiled=True)
    pair_qkv = store_qkv[cand_passage]
    pair_lengths = jnp.sum(jnp.isfinite(pair_qkv[:, :, 0, head_dim]).astype(jnp.int32), axis=1)
    query_attn = attend_queries(query_qkv, head_dim)
    passage_attn = attend_pairs(query_qkv, pair_qkv, pair_lengths, head_dim, cands)
    return (query_attn, passage_attn)


def solution(mesh):
    in_specs = (
        P("store", None, "tp"),
        P("store", None, "tp"),
        P("store"),
        P("store"),
        P(),
        P(None, "tp", None),
    )
    out_specs = (P("store", None, "tp"), P("store", None, "tp"))
    return jax.shard_map(local, mesh=mesh, in_specs=in_specs, out_specs=out_specs, check_vma=False)
```

```python
import math

import jax
import jax.numpy as jnp
from jax import lax
from jax.sharding import PartitionSpec as P


def rms_rows(rows, norm_gain):
    values = rows.astype(jnp.float32)
    meansq = jnp.mean(values * values, axis=-1, keepdims=True)
    scaled = values * lax.rsqrt(meansq + 1e-05) * norm_gain.astype(jnp.float32)
    return scaled.astype(jnp.bfloat16)


def rotate_parts(raw, positions, head_dim):
    half_dim = head_dim // 2
    inverse = jnp.exp(
        jnp.arange(half_dim, dtype=jnp.float32) * (-2.0 * math.log(10000.0) / head_dim)
    )
    angles = positions[:, None] * inverse[None, :]
    cosine = jnp.cos(angles)[:, None, :]
    sine_part = jnp.sin(angles)[:, None, :]

    def turned(block):
        first = block[..., :half_dim]
        second = block[..., half_dim:]
        return jnp.concatenate(
            [first * cosine - second * sine_part, second * cosine + first * sine_part], axis=-1
        )

    queries = turned(raw[..., :head_dim])
    keyset = turned(raw[..., head_dim : 2 * head_dim])
    values = raw[..., 2 * head_dim :]
    return jnp.concatenate([queries, keyset, values], axis=-1).astype(jnp.bfloat16)


def softmax_rounded(scores, allowed):
    masked = jnp.where(allowed, scores, jnp.float32(-1e30))
    peak = jnp.max(masked, axis=-1, keepdims=True)
    expon = jnp.where(allowed, jnp.exp(masked - peak), jnp.float32(0.0))
    return (expon / jnp.sum(expon, axis=-1, keepdims=True)).astype(jnp.bfloat16)


def attend_queries(query_qkv, head_dim):
    count, query_len, heads = (query_qkv.shape[0], query_qkv.shape[1], query_qkv.shape[2])
    scale = head_dim ** (-0.5)
    scores = (
        jnp.einsum(
            "bqhd,bkhd->bhqk",
            query_qkv[..., :head_dim],
            query_qkv[..., head_dim : 2 * head_dim],
            preferred_element_type=jnp.float32,
        )
        * scale
    )
    steps_row = jnp.arange(query_len, dtype=jnp.int32)
    allowed = steps_row[:, None] >= steps_row[None, :]
    weights = softmax_rounded(scores, allowed[None, None])
    output = jnp.einsum(
        "bhqk,bkhd->bqhd",
        weights,
        query_qkv[..., 2 * head_dim :],
        preferred_element_type=jnp.float32,
    )
    return output.reshape(count, query_len, heads * head_dim).astype(jnp.bfloat16)


def attend_core(query_kv, pair_qkv, pair_lengths, head_dim):
    query_len = query_kv.shape[1]
    pairs, passage_len, heads = (pair_qkv.shape[0], pair_qkv.shape[1], pair_qkv.shape[2])
    scale = head_dim ** (-0.5)
    keyset = jnp.concatenate(
        [query_kv[..., :head_dim], pair_qkv[..., head_dim : 2 * head_dim]], axis=1
    )
    values = jnp.concatenate([query_kv[..., head_dim:], pair_qkv[..., 2 * head_dim :]], axis=1)
    scores = (
        jnp.einsum(
            "bihd,bthd->bhit", pair_qkv[..., :head_dim], keyset, preferred_element_type=jnp.float32
        )
        * scale
    )
    column = jnp.arange(query_len + passage_len, dtype=jnp.int32) - query_len
    row_index = jnp.arange(passage_len, dtype=jnp.int32)
    allowed = (column[None, None, :] < 0) | (column[None, None, :] <= row_index[None, :, None]) & (
        column[None, None, :] < pair_lengths[:, None, None]
    )
    weights = softmax_rounded(scores, allowed[:, None])
    output = jnp.einsum("bhit,bthd->bihd", weights, values, preferred_element_type=jnp.float32)
    live = row_index[None, :] < pair_lengths[:, None]
    output = jnp.where(live[:, :, None, None], output, jnp.float32(0.0))
    return output.reshape(pairs, passage_len, heads * head_dim).astype(jnp.bfloat16)


def attend_pairs(query_qkv, pair_qkv, pair_lengths, head_dim, cands):
    repeated = jnp.repeat(query_qkv[..., head_dim:], cands, axis=0)
    return attend_core(repeated, pair_qkv, pair_lengths, head_dim)


def gather_store(own):
    n_store = lax.axis_size("store")
    count = own.shape[0]
    if n_store > 8 or n_store % 2:
        return lax.all_gather(own, "store", axis=0, tiled=True), lambda rows: rows
    ring = [s for s in range(0, n_store, 2)] + [s for s in range(n_store - 1, 0, -2)]
    place = [0] * n_store
    for i, s in enumerate(ring):
        place[s] = i
    forward = [(ring[i], ring[(i + 1) % n_store]) for i in range(n_store)]
    backward = [(ring[(i + 1) % n_store], ring[i]) for i in range(n_store)]
    parts = [own]
    ahead = own
    for _ in range(n_store // 2):
        ahead = lax.ppermute(ahead, "store", forward)
        parts.append(ahead)
    behind = own
    for _ in range((n_store - 1) // 2):
        behind = lax.ppermute(behind, "store", backward)
        parts.append(behind)
    place_of = jnp.asarray(place, dtype=jnp.int32)
    mine = place_of[lax.axis_index("store")]

    def rows_of(rows):
        dist = (place_of[rows // count] - mine) % n_store
        slot = jnp.where(dist == 0, 0, jnp.where(dist < n_store // 2, n_store // 2 + dist, n_store - dist))
        return slot * count + rows % count

    return jnp.concatenate(parts, axis=0), rows_of


def local(query_embeds, passage_embeds, passage_lengths, cand_passage, norm_gain, w_qkv):
    quer_count, query_len, width_part = query_embeds.shape
    pass_count, passage_len = (passage_embeds.shape[0], passage_embeds.shape[1])
    pairs_dev = cand_passage.shape[0]
    cands = pairs_dev // quer_count
    heads_part = w_qkv.shape[1]
    head_dim = w_qkv.shape[2] // 3
    query_rows = query_embeds.reshape(quer_count * query_len, width_part)
    passage_rows = passage_embeds.reshape(pass_count * passage_len, width_part)
    query_pos = jnp.tile(jnp.arange(query_len, dtype=jnp.float32), quer_count)
    passage_pos = query_len + jnp.tile(jnp.arange(passage_len, dtype=jnp.float32), pass_count)
    query_total = quer_count * query_len
    all_rows = jnp.concatenate([query_rows, passage_rows], axis=0)
    full_rows = lax.all_gather(all_rows, "tp", axis=1, tiled=True)
    normed = rms_rows(full_rows, norm_gain)
    raw = jnp.einsum("nk,khc->nhc", normed, w_qkv, preferred_element_type=jnp.float32)
    projected = rotate_parts(raw, jnp.concatenate([query_pos, passage_pos], axis=0), head_dim)
    query_qkv = projected[:query_total].reshape(quer_count, query_len, heads_part, 3 * head_dim)
    own_qkv = projected[query_total:].reshape(pass_count, passage_len, heads_part, 3 * head_dim)
    padded = jnp.arange(passage_len, dtype=jnp.int32)[None, :] >= passage_lengths[:, None]
    head_at = lax.broadcasted_iota(jnp.int32, own_qkv.shape, 2)
    col_at = lax.broadcasted_iota(jnp.int32, own_qkv.shape, 3)
    mark = padded[:, :, None, None] & (head_at == 0) & (col_at == head_dim)
    own_qkv = jnp.where(mark, jnp.asarray(jnp.inf, own_qkv.dtype), own_qkv)
    store_qkv, rows_of = gather_store(own_qkv)
    pair_qkv = store_qkv[rows_of(cand_passage)]
    pair_lengths = jnp.sum(jnp.isfinite(pair_qkv[:, :, 0, head_dim]).astype(jnp.int32), axis=1)
    query_attn = attend_queries(query_qkv, head_dim)
    passage_attn = attend_pairs(query_qkv, pair_qkv, pair_lengths, head_dim, cands)
    return (query_attn, passage_attn)


def solution(mesh):
    in_specs = (
        P("store", None, "tp"),
        P("store", None, "tp"),
        P("store"),
        P("store"),
        P(),
        P(None, "tp", None),
    )
    out_specs = (P("store", None, "tp"), P("store", None, "tp"))
    return jax.shard_map(local, mesh=mesh, in_specs=in_specs, out_specs=out_specs, check_vma=False)
```

```python
import math

import jax
import jax.numpy as jnp
from jax import lax
from jax.sharding import PartitionSpec as P


def rms_rows(rows, norm_gain):
    values = rows.astype(jnp.float32)
    meansq = jnp.mean(values * values, axis=-1, keepdims=True)
    scaled = values * lax.rsqrt(meansq + 1e-05) * norm_gain.astype(jnp.float32)
    return scaled.astype(jnp.bfloat16)


def rotate_parts(raw, positions, head_dim):
    half_dim = head_dim // 2
    inverse = jnp.exp(
        jnp.arange(half_dim, dtype=jnp.float32) * (-2.0 * math.log(10000.0) / head_dim)
    )
    angles = positions[:, None] * inverse[None, :]
    cosine = jnp.cos(angles)[:, None, :]
    sine_part = jnp.sin(angles)[:, None, :]

    def turned(block):
        first = block[..., :half_dim]
        second = block[..., half_dim:]
        return jnp.concatenate(
            [first * cosine - second * sine_part, second * cosine + first * sine_part], axis=-1
        )

    queries = turned(raw[..., :head_dim])
    keyset = turned(raw[..., head_dim : 2 * head_dim])
    values = raw[..., 2 * head_dim :]
    return jnp.concatenate([queries, keyset, values], axis=-1).astype(jnp.bfloat16)


def softmax_rounded(scores, allowed):
    masked = jnp.where(allowed, scores, jnp.float32(-1e30))
    peak = jnp.max(masked, axis=-1, keepdims=True)
    expon = jnp.where(allowed, jnp.exp(masked - peak), jnp.float32(0.0))
    return (expon / jnp.sum(expon, axis=-1, keepdims=True)).astype(jnp.bfloat16)


def attend_queries(query_qkv, head_dim):
    count, query_len, heads = (query_qkv.shape[0], query_qkv.shape[1], query_qkv.shape[2])
    scale = head_dim ** (-0.5)
    scores = (
        jnp.einsum(
            "bqhd,bkhd->bhqk",
            query_qkv[..., :head_dim],
            query_qkv[..., head_dim : 2 * head_dim],
            preferred_element_type=jnp.float32,
        )
        * scale
    )
    steps_row = jnp.arange(query_len, dtype=jnp.int32)
    allowed = steps_row[:, None] >= steps_row[None, :]
    weights = softmax_rounded(scores, allowed[None, None])
    output = jnp.einsum(
        "bhqk,bkhd->bqhd",
        weights,
        query_qkv[..., 2 * head_dim :],
        preferred_element_type=jnp.float32,
    )
    return output.reshape(count, query_len, heads * head_dim).astype(jnp.bfloat16)


def attend_core(query_kv, pair_qkv, pair_lengths, head_dim):
    query_len = query_kv.shape[1]
    pairs, passage_len, heads = (pair_qkv.shape[0], pair_qkv.shape[1], pair_qkv.shape[2])
    scale = head_dim ** (-0.5)
    keyset = jnp.concatenate(
        [query_kv[..., :head_dim], pair_qkv[..., head_dim : 2 * head_dim]], axis=1
    )
    values = jnp.concatenate([query_kv[..., head_dim:], pair_qkv[..., 2 * head_dim :]], axis=1)
    scores = (
        jnp.einsum(
            "bihd,bthd->bhit", pair_qkv[..., :head_dim], keyset, preferred_element_type=jnp.float32
        )
        * scale
    )
    column = jnp.arange(query_len + passage_len, dtype=jnp.int32) - query_len
    row_index = jnp.arange(passage_len, dtype=jnp.int32)
    allowed = (column[None, None, :] < 0) | (column[None, None, :] <= row_index[None, :, None]) & (
        column[None, None, :] < pair_lengths[:, None, None]
    )
    weights = softmax_rounded(scores, allowed[:, None])
    output = jnp.einsum("bhit,bthd->bihd", weights, values, preferred_element_type=jnp.float32)
    live = row_index[None, :] < pair_lengths[:, None]
    output = jnp.where(live[:, :, None, None], output, jnp.float32(0.0))
    return output.reshape(pairs, passage_len, heads * head_dim).astype(jnp.bfloat16)


def attend_pairs(query_qkv, pair_qkv, pair_lengths, head_dim, cands):
    repeated = jnp.repeat(query_qkv[..., head_dim:], cands, axis=0)
    return attend_core(repeated, pair_qkv, pair_lengths, head_dim)


def gather_store(own):
    n_store = lax.axis_size("store")
    count = own.shape[0]
    if n_store > 8 or n_store % 2:
        return lax.all_gather(own, "store", axis=0, tiled=True), lambda rows: rows
    ring = [s for s in range(0, n_store, 2)] + [s for s in range(n_store - 1, 0, -2)]
    place = [0] * n_store
    for i, s in enumerate(ring):
        place[s] = i
    forward = [(ring[i], ring[(i + 1) % n_store]) for i in range(n_store)]
    backward = [(ring[(i + 1) % n_store], ring[i]) for i in range(n_store)]
    parts = [own]
    ahead = own
    for _ in range(n_store // 2):
        ahead = lax.ppermute(ahead, "store", forward)
        parts.append(ahead)
    behind = own
    for _ in range((n_store - 1) // 2):
        behind = lax.ppermute(behind, "store", backward)
        parts.append(behind)
    place_of = jnp.asarray(place, dtype=jnp.int32)
    mine = place_of[lax.axis_index("store")]

    def rows_of(rows):
        dist = (place_of[rows // count] - mine) % n_store
        slot = jnp.where(dist == 0, 0, jnp.where(dist < n_store // 2, n_store // 2 + dist, n_store - dist))
        return slot * count + rows % count

    return jnp.concatenate(parts, axis=0), rows_of


def local(query_embeds, passage_embeds, passage_lengths_in, cand_passage, norm_gain, w_qkv):
    quer_count, query_len, width_part = query_embeds.shape
    pass_count, passage_len = (passage_embeds.shape[0], passage_embeds.shape[1])
    pairs_dev = cand_passage.shape[0]
    cands = pairs_dev // quer_count
    heads_part = w_qkv.shape[1]
    head_dim = w_qkv.shape[2] // 3
    query_rows = query_embeds.reshape(quer_count * query_len, width_part)
    passage_rows = passage_embeds.reshape(pass_count * passage_len, width_part)
    query_pos = jnp.tile(jnp.arange(query_len, dtype=jnp.float32), quer_count)
    passage_pos = query_len + jnp.tile(jnp.arange(passage_len, dtype=jnp.float32), pass_count)
    query_total = quer_count * query_len
    all_rows = jnp.concatenate([query_rows, passage_rows], axis=0)
    full_rows = lax.all_gather(all_rows, "tp", axis=1, tiled=True)
    normed = rms_rows(full_rows, norm_gain)
    positions = jnp.concatenate([query_pos, passage_pos], axis=0)
    groups = 2 if heads_part % 2 == 0 else 1
    per_group = heads_part // groups
    query_outs, pair_outs = [], []
    pair_lengths = None
    for group in range(groups):
        w_part = w_qkv[:, group * per_group : (group + 1) * per_group, :]
        raw = jnp.einsum("nk,khc->nhc", normed, w_part, preferred_element_type=jnp.float32)
        projected = rotate_parts(raw, positions, head_dim)
        query_qkv = projected[:query_total].reshape(quer_count, query_len, per_group, 3 * head_dim)
        own_qkv = projected[query_total:].reshape(pass_count, passage_len, per_group, 3 * head_dim)
        if group == 0:
            padded = jnp.arange(passage_len, dtype=jnp.int32)[None, :] >= passage_lengths_in[:, None]
            head_at = lax.broadcasted_iota(jnp.int32, own_qkv.shape, 2)
            col_at = lax.broadcasted_iota(jnp.int32, own_qkv.shape, 3)
            mark = padded[:, :, None, None] & (head_at == 0) & (col_at == head_dim)
            own_qkv = jnp.where(mark, jnp.asarray(jnp.inf, own_qkv.dtype), own_qkv)
        store_qkv, rows_of = gather_store(own_qkv)
        pair_qkv = store_qkv[rows_of(cand_passage)]
        if group == 0:
            pair_lengths = jnp.sum(jnp.isfinite(pair_qkv[:, :, 0, head_dim]).astype(jnp.int32), axis=1)
        query_outs.append(attend_queries(query_qkv, head_dim))
        pair_outs.append(attend_pairs(query_qkv, pair_qkv, pair_lengths, head_dim, cands))
    query_attn = jnp.concatenate(query_outs, axis=-1)
    passage_attn = jnp.concatenate(pair_outs, axis=-1)
    return (query_attn, passage_attn)


def solution(mesh):
    in_specs = (
        P("store", None, "tp"),
        P("store", None, "tp"),
        P("store"),
        P("store"),
        P(),
        P(None, "tp", None),
    )
    out_specs = (P("store", None, "tp"), P("store", None, "tp"))
    return jax.shard_map(local, mesh=mesh, in_specs=in_specs, out_specs=out_specs, check_vma=False)
```

```python
import math

import jax
import jax.numpy as jnp
from jax import lax
from jax.sharding import PartitionSpec as P


def rms_rows(rows, norm_gain):
    values = rows.astype(jnp.float32)
    meansq = jnp.mean(values * values, axis=-1, keepdims=True)
    scaled = values * lax.rsqrt(meansq + 1e-05) * norm_gain.astype(jnp.float32)
    return scaled.astype(jnp.bfloat16)


def rotate_parts(raw, positions, head_dim):
    half_dim = head_dim // 2
    inverse = jnp.exp(
        jnp.arange(half_dim, dtype=jnp.float32) * (-2.0 * math.log(10000.0) / head_dim)
    )
    angles = positions[:, None] * inverse[None, :]
    cosine = jnp.cos(angles)[:, None, :]
    sine_part = jnp.sin(angles)[:, None, :]

    def turned(block):
        first = block[..., :half_dim]
        second = block[..., half_dim:]
        return jnp.concatenate(
            [first * cosine - second * sine_part, second * cosine + first * sine_part], axis=-1
        )

    queries = turned(raw[..., :head_dim])
    keyset = turned(raw[..., head_dim : 2 * head_dim])
    values = raw[..., 2 * head_dim :]
    return jnp.concatenate([queries, keyset, values], axis=-1).astype(jnp.bfloat16)


def softmax_rounded(scores, allowed):
    masked = jnp.where(allowed, scores, jnp.float32(-1e30))
    peak = jnp.max(masked, axis=-1, keepdims=True)
    expon = jnp.where(allowed, jnp.exp(masked - peak), jnp.float32(0.0))
    return (expon / jnp.sum(expon, axis=-1, keepdims=True)).astype(jnp.bfloat16)


def attend_queries(query_qkv, head_dim):
    count, query_len, heads = (query_qkv.shape[0], query_qkv.shape[1], query_qkv.shape[2])
    scale = head_dim ** (-0.5)
    scores = (
        jnp.einsum(
            "bqhd,bkhd->bhqk",
            query_qkv[..., :head_dim],
            query_qkv[..., head_dim : 2 * head_dim],
            preferred_element_type=jnp.float32,
        )
        * scale
    )
    steps_row = jnp.arange(query_len, dtype=jnp.int32)
    allowed = steps_row[:, None] >= steps_row[None, :]
    weights = softmax_rounded(scores, allowed[None, None])
    output = jnp.einsum(
        "bhqk,bkhd->bqhd",
        weights,
        query_qkv[..., 2 * head_dim :],
        preferred_element_type=jnp.float32,
    )
    return output.reshape(count, query_len, heads * head_dim).astype(jnp.bfloat16)


def attend_core(query_kv, pair_qkv, pair_lengths, head_dim):
    query_len = query_kv.shape[1]
    pairs, passage_len, heads = (pair_qkv.shape[0], pair_qkv.shape[1], pair_qkv.shape[2])
    scale = head_dim ** (-0.5)
    keyset = jnp.concatenate(
        [query_kv[..., :head_dim], pair_qkv[..., head_dim : 2 * head_dim]], axis=1
    )
    values = jnp.concatenate([query_kv[..., head_dim:], pair_qkv[..., 2 * head_dim :]], axis=1)
    scores = (
        jnp.einsum(
            "bihd,bthd->bhit", pair_qkv[..., :head_dim], keyset, preferred_element_type=jnp.float32
        )
        * scale
    )
    column = jnp.arange(query_len + passage_len, dtype=jnp.int32) - query_len
    row_index = jnp.arange(passage_len, dtype=jnp.int32)
    allowed = (column[None, None, :] < 0) | (column[None, None, :] <= row_index[None, :, None]) & (
        column[None, None, :] < pair_lengths[:, None, None]
    )
    weights = softmax_rounded(scores, allowed[:, None])
    output = jnp.einsum("bhit,bthd->bihd", weights, values, preferred_element_type=jnp.float32)
    live = row_index[None, :] < pair_lengths[:, None]
    output = jnp.where(live[:, :, None, None], output, jnp.float32(0.0))
    return output.reshape(pairs, passage_len, heads * head_dim).astype(jnp.bfloat16)


def attend_pairs(query_qkv, pair_qkv, pair_lengths, head_dim, cands):
    repeated = jnp.repeat(query_qkv[..., head_dim:], cands, axis=0)
    return attend_core(repeated, pair_qkv, pair_lengths, head_dim)


def gather_store(own):
    n_store = lax.axis_size("store")
    count = own.shape[0]
    if n_store > 8 or n_store % 2:
        return lax.all_gather(own, "store", axis=0, tiled=True), lambda rows: rows
    ring = [s for s in range(0, n_store, 2)] + [s for s in range(n_store - 1, 0, -2)]
    place = [0] * n_store
    for i, s in enumerate(ring):
        place[s] = i
    forward = [(ring[i], ring[(i + 1) % n_store]) for i in range(n_store)]
    backward = [(ring[(i + 1) % n_store], ring[i]) for i in range(n_store)]
    steps = []
    pieces = []
    for row in range(count):
        ahead_steps = n_store // 2 if row % 2 == 0 else (n_store - 1) // 2
        behind_steps = n_store - 1 - ahead_steps
        steps.append((ahead_steps, behind_steps))
        piece = own[row : row + 1]
        parts = [piece]
        ahead = piece
        behind = piece
        for k in range(max(ahead_steps, behind_steps)):
            if k < ahead_steps:
                ahead = lax.ppermute(ahead, "store", forward)
                parts.append(ahead)
            if k < behind_steps:
                behind = lax.ppermute(behind, "store", backward)
                parts.append(behind)
        pieces.append(parts)
    ordered = []
    for row in range(count):
        ahead_steps, behind_steps = steps[row]
        parts = pieces[row]
        got_ahead, got_behind = [], []
        at = 1
        for k in range(max(ahead_steps, behind_steps)):
            if k < ahead_steps:
                got_ahead.append(parts[at])
                at += 1
            if k < behind_steps:
                got_behind.append(parts[at])
                at += 1
        ordered.extend([parts[0]] + got_ahead + got_behind)
    place_of = jnp.asarray(place, dtype=jnp.int32)
    mine = place_of[lax.axis_index("store")]
    ahead_of = jnp.asarray([s[0] for s in steps], dtype=jnp.int32)

    def rows_of(rows):
        dist = (place_of[rows // count] - mine) % n_store
        row = rows % count
        first = ahead_of[row]
        slot = jnp.where(dist == 0, 0, jnp.where(dist < n_store - first, first + dist, n_store - dist))
        return row * n_store + slot

    return jnp.concatenate(ordered, axis=0), rows_of


def local(query_embeds, passage_embeds, passage_lengths, cand_passage, norm_gain, w_qkv):
    quer_count, query_len, width_part = query_embeds.shape
    pass_count, passage_len = (passage_embeds.shape[0], passage_embeds.shape[1])
    pairs_dev = cand_passage.shape[0]
    cands = pairs_dev // quer_count
    heads_part = w_qkv.shape[1]
    head_dim = w_qkv.shape[2] // 3
    query_rows = query_embeds.reshape(quer_count * query_len, width_part)
    passage_rows = passage_embeds.reshape(pass_count * passage_len, width_part)
    query_pos = jnp.tile(jnp.arange(query_len, dtype=jnp.float32), quer_count)
    passage_pos = query_len + jnp.tile(jnp.arange(passage_len, dtype=jnp.float32), pass_count)
    query_total = quer_count * query_len
    all_rows = jnp.concatenate([query_rows, passage_rows], axis=0)
    full_rows = lax.all_gather(all_rows, "tp", axis=1, tiled=True)
    normed = rms_rows(full_rows, norm_gain)
    raw = jnp.einsum("nk,khc->nhc", normed, w_qkv, preferred_element_type=jnp.float32)
    projected = rotate_parts(raw, jnp.concatenate([query_pos, passage_pos], axis=0), head_dim)
    query_qkv = projected[:query_total].reshape(quer_count, query_len, heads_part, 3 * head_dim)
    own_qkv = projected[query_total:].reshape(pass_count, passage_len, heads_part, 3 * head_dim)
    padded = jnp.arange(passage_len, dtype=jnp.int32)[None, :] >= passage_lengths[:, None]
    head_at = lax.broadcasted_iota(jnp.int32, own_qkv.shape, 2)
    col_at = lax.broadcasted_iota(jnp.int32, own_qkv.shape, 3)
    mark = padded[:, :, None, None] & (head_at == 0) & (col_at == head_dim)
    own_qkv = jnp.where(mark, jnp.asarray(jnp.inf, own_qkv.dtype), own_qkv)
    store_qkv, rows_of = gather_store(own_qkv)
    pair_qkv = store_qkv[rows_of(cand_passage)]
    pair_lengths = jnp.sum(jnp.isfinite(pair_qkv[:, :, 0, head_dim]).astype(jnp.int32), axis=1)
    query_attn = attend_queries(query_qkv, head_dim)
    passage_attn = attend_pairs(query_qkv, pair_qkv, pair_lengths, head_dim, cands)
    return (query_attn, passage_attn)


def solution(mesh):
    in_specs = (
        P("store", None, "tp"),
        P("store", None, "tp"),
        P("store"),
        P("store"),
        P(),
        P(None, "tp", None),
    )
    out_specs = (P("store", None, "tp"), P("store", None, "tp"))
    return jax.shard_map(local, mesh=mesh, in_specs=in_specs, out_specs=out_specs, check_vma=False)
```

```python
import math

import jax
import jax.numpy as jnp
from jax import lax
from jax.sharding import PartitionSpec as P


def rms_rows(rows, norm_gain):
    values = rows.astype(jnp.float32)
    meansq = jnp.mean(values * values, axis=-1, keepdims=True)
    scaled = values * lax.rsqrt(meansq + 1e-05) * norm_gain.astype(jnp.float32)
    return scaled.astype(jnp.bfloat16)


def rotate_parts(raw, positions, head_dim):
    half_dim = head_dim // 2
    inverse = jnp.exp(
        jnp.arange(half_dim, dtype=jnp.float32) * (-2.0 * math.log(10000.0) / head_dim)
    )
    angles = positions[:, None] * inverse[None, :]
    cosine = jnp.cos(angles)[:, None, :]
    sine_part = jnp.sin(angles)[:, None, :]

    def turned(block):
        first = block[..., :half_dim]
        second = block[..., half_dim:]
        return jnp.concatenate(
            [first * cosine - second * sine_part, second * cosine + first * sine_part], axis=-1
        )

    queries = turned(raw[..., :head_dim])
    keyset = turned(raw[..., head_dim : 2 * head_dim])
    values = raw[..., 2 * head_dim :]
    return jnp.concatenate([queries, keyset, values], axis=-1).astype(jnp.bfloat16)


def softmax_rounded(scores, allowed):
    masked = jnp.where(allowed, scores, jnp.float32(-1e30))
    peak = jnp.max(masked, axis=-1, keepdims=True)
    expon = jnp.where(allowed, jnp.exp(masked - peak), jnp.float32(0.0))
    return (expon / jnp.sum(expon, axis=-1, keepdims=True)).astype(jnp.bfloat16)


def attend_queries(query_qkv, head_dim):
    count, query_len, heads = (query_qkv.shape[0], query_qkv.shape[1], query_qkv.shape[2])
    scale = head_dim ** (-0.5)
    scores = (
        jnp.einsum(
            "bqhd,bkhd->bhqk",
            query_qkv[..., :head_dim],
            query_qkv[..., head_dim : 2 * head_dim],
            preferred_element_type=jnp.float32,
        )
        * scale
    )
    steps_row = jnp.arange(query_len, dtype=jnp.int32)
    allowed = steps_row[:, None] >= steps_row[None, :]
    weights = softmax_rounded(scores, allowed[None, None])
    output = jnp.einsum(
        "bhqk,bkhd->bqhd",
        weights,
        query_qkv[..., 2 * head_dim :],
        preferred_element_type=jnp.float32,
    )
    return output.reshape(count, query_len, heads * head_dim).astype(jnp.bfloat16)


def attend_core(query_kv, pair_qkv, pair_lengths, head_dim):
    query_len = query_kv.shape[1]
    pairs, passage_len, heads = (pair_qkv.shape[0], pair_qkv.shape[1], pair_qkv.shape[2])
    scale = head_dim ** (-0.5)
    keyset = jnp.concatenate(
        [query_kv[..., :head_dim], pair_qkv[..., head_dim : 2 * head_dim]], axis=1
    )
    values = jnp.concatenate([query_kv[..., head_dim:], pair_qkv[..., 2 * head_dim :]], axis=1)
    scores = (
        jnp.einsum(
            "bihd,bthd->bhit", pair_qkv[..., :head_dim], keyset, preferred_element_type=jnp.float32
        )
        * scale
    )
    column = jnp.arange(query_len + passage_len, dtype=jnp.int32) - query_len
    row_index = jnp.arange(passage_len, dtype=jnp.int32)
    allowed = (column[None, None, :] < 0) | (column[None, None, :] <= row_index[None, :, None]) & (
        column[None, None, :] < pair_lengths[:, None, None]
    )
    weights = softmax_rounded(scores, allowed[:, None])
    output = jnp.einsum("bhit,bthd->bihd", weights, values, preferred_element_type=jnp.float32)
    live = row_index[None, :] < pair_lengths[:, None]
    output = jnp.where(live[:, :, None, None], output, jnp.float32(0.0))
    return output.reshape(pairs, passage_len, heads * head_dim).astype(jnp.bfloat16)


def attend_pairs(query_qkv, pair_qkv, pair_lengths, head_dim, cands):
    repeated = jnp.repeat(query_qkv[..., head_dim:], cands, axis=0)
    return attend_core(repeated, pair_qkv, pair_lengths, head_dim)


def ring_steps(own):
    n_store = lax.axis_size("store")
    ring = [s for s in range(0, n_store, 2)] + [s for s in range(n_store - 1, 0, -2)]
    place = [0] * n_store
    for i, s in enumerate(ring):
        place[s] = i
    forward = [(ring[i], ring[(i + 1) % n_store]) for i in range(n_store)]
    backward = [(ring[(i + 1) % n_store], ring[i]) for i in range(n_store)]
    groups = [([own], [0])]
    ahead = own
    behind = own
    for k in range(1, n_store // 2 + 1):
        blocks, dists = [], []
        ahead = lax.ppermute(ahead, "store", forward)
        blocks.append(ahead)
        dists.append(n_store - k)
        if k <= (n_store - 1) // 2:
            behind = lax.ppermute(behind, "store", backward)
            blocks.append(behind)
            dists.append(k)
        groups.append((blocks, dists))
    return groups, jnp.asarray(place, dtype=jnp.int32)


def attend_arrived(query_qkv, blocks, head_dim):
    passages = jnp.concatenate(blocks, axis=0) if len(blocks) > 1 else blocks[0]
    lengths = jnp.sum(jnp.isfinite(passages[:, :, 0, head_dim]).astype(jnp.int32), axis=1)
    count = passages.shape[0]
    quer_count = query_qkv.shape[0]
    query_kv = jnp.repeat(query_qkv[..., head_dim:], count, axis=0)
    pair_qkv = jnp.tile(passages, (quer_count, 1, 1, 1))
    return attend_core(query_kv, pair_qkv, jnp.tile(lengths, quer_count), head_dim)


def local(query_embeds, passage_embeds, passage_lengths, cand_passage, norm_gain, w_qkv):
    quer_count, query_len, width_part = query_embeds.shape
    pass_count, passage_len = (passage_embeds.shape[0], passage_embeds.shape[1])
    pairs_dev = cand_passage.shape[0]
    cands = pairs_dev // quer_count
    heads_part = w_qkv.shape[1]
    head_dim = w_qkv.shape[2] // 3
    query_rows = query_embeds.reshape(quer_count * query_len, width_part)
    passage_rows = passage_embeds.reshape(pass_count * passage_len, width_part)
    query_pos = jnp.tile(jnp.arange(query_len, dtype=jnp.float32), quer_count)
    passage_pos = query_len + jnp.tile(jnp.arange(passage_len, dtype=jnp.float32), pass_count)
    query_total = quer_count * query_len
    all_rows = jnp.concatenate([query_rows, passage_rows], axis=0)
    full_rows = lax.all_gather(all_rows, "tp", axis=1, tiled=True)
    normed = rms_rows(full_rows, norm_gain)
    raw = jnp.einsum("nk,khc->nhc", normed, w_qkv, preferred_element_type=jnp.float32)
    projected = rotate_parts(raw, jnp.concatenate([query_pos, passage_pos], axis=0), head_dim)
    query_qkv = projected[:query_total].reshape(quer_count, query_len, heads_part, 3 * head_dim)
    own_qkv = projected[query_total:].reshape(pass_count, passage_len, heads_part, 3 * head_dim)
    padded = jnp.arange(passage_len, dtype=jnp.int32)[None, :] >= passage_lengths[:, None]
    head_at = lax.broadcasted_iota(jnp.int32, own_qkv.shape, 2)
    col_at = lax.broadcasted_iota(jnp.int32, own_qkv.shape, 3)
    mark = padded[:, :, None, None] & (head_at == 0) & (col_at == head_dim)
    own_qkv = jnp.where(mark, jnp.asarray(jnp.inf, own_qkv.dtype), own_qkv)
    query_attn = attend_queries(query_qkv, head_dim)
    n_store = lax.axis_size("store")
    if n_store > 8 or n_store % 2:
        store_qkv = lax.all_gather(own_qkv, "store", axis=0, tiled=True)
        pair_qkv = store_qkv[cand_passage]
        pair_lengths = jnp.sum(jnp.isfinite(pair_qkv[:, :, 0, head_dim]).astype(jnp.int32), axis=1)
        passage_attn = attend_pairs(query_qkv, pair_qkv, pair_lengths, head_dim, cands)
        return (query_attn, passage_attn)
    groups, place_of = ring_steps(own_qkv)
    outs = []
    first_row = [0] * n_store
    width = [0] * n_store
    within = [0] * n_store
    row = 0
    for blocks, dists in groups:
        outs.append(attend_arrived(query_qkv, blocks, head_dim))
        for i, dist in enumerate(dists):
            first_row[dist] = row
            width[dist] = len(dists) * pass_count
            within[dist] = i * pass_count
        row += quer_count * len(dists) * pass_count
    every = jnp.concatenate(outs, axis=0)
    mine = place_of[lax.axis_index("store")]
    dist = (place_of[cand_passage // pass_count] - mine) % n_store
    own_query = jnp.arange(pairs_dev, dtype=jnp.int32) // cands
    pick = (
        jnp.asarray(first_row, dtype=jnp.int32)[dist]
        + own_query * jnp.asarray(width, dtype=jnp.int32)[dist]
        + jnp.asarray(within, dtype=jnp.int32)[dist]
        + cand_passage % pass_count
    )
    passage_attn = every[pick]
    return (query_attn, passage_attn)


def solution(mesh):
    in_specs = (
        P("store", None, "tp"),
        P("store", None, "tp"),
        P("store"),
        P("store"),
        P(),
        P(None, "tp", None),
    )
    out_specs = (P("store", None, "tp"), P("store", None, "tp"))
    return jax.shard_map(local, mesh=mesh, in_specs=in_specs, out_specs=out_specs, check_vma=False)
```

```python
import functools
import math

import jax
import jax.numpy as jnp
from jax import lax
from jax.experimental import pallas as pl
from jax.sharding import PartitionSpec as P


def rms_rows(rows, norm_gain):
    values = rows.astype(jnp.float32)
    meansq = jnp.mean(values * values, axis=-1, keepdims=True)
    scaled = values * lax.rsqrt(meansq + 1e-05) * norm_gain.astype(jnp.float32)
    return scaled.astype(jnp.bfloat16)


def rotate_parts(raw, positions, head_dim):
    half_dim = head_dim // 2
    inverse = jnp.exp(
        jnp.arange(half_dim, dtype=jnp.float32) * (-2.0 * math.log(10000.0) / head_dim)
    )
    angles = positions[:, None] * inverse[None, :]
    cosine = jnp.cos(angles)[:, None, :]
    sine_part = jnp.sin(angles)[:, None, :]

    def turned(block):
        first = block[..., :half_dim]
        second = block[..., half_dim:]
        return jnp.concatenate(
            [first * cosine - second * sine_part, second * cosine + first * sine_part], axis=-1
        )

    queries = turned(raw[..., :head_dim])
    keyset = turned(raw[..., head_dim : 2 * head_dim])
    values = raw[..., 2 * head_dim :]
    return jnp.concatenate([queries, keyset, values], axis=-1).astype(jnp.bfloat16)


def softmax_rounded(scores, allowed):
    masked = jnp.where(allowed, scores, jnp.float32(-1e30))
    peak = jnp.max(masked, axis=-1, keepdims=True)
    expon = jnp.where(allowed, jnp.exp(masked - peak), jnp.float32(0.0))
    return (expon / jnp.sum(expon, axis=-1, keepdims=True)).astype(jnp.bfloat16)


def attend_queries(query_qkv, head_dim):
    count, query_len, heads = (query_qkv.shape[0], query_qkv.shape[1], query_qkv.shape[2])
    scale = head_dim ** (-0.5)
    scores = (
        jnp.einsum(
            "bqhd,bkhd->bhqk",
            query_qkv[..., :head_dim],
            query_qkv[..., head_dim : 2 * head_dim],
            preferred_element_type=jnp.float32,
        )
        * scale
    )
    steps_row = jnp.arange(query_len, dtype=jnp.int32)
    allowed = steps_row[:, None] >= steps_row[None, :]
    weights = softmax_rounded(scores, allowed[None, None])
    output = jnp.einsum(
        "bhqk,bkhd->bqhd",
        weights,
        query_qkv[..., 2 * head_dim :],
        preferred_element_type=jnp.float32,
    )
    return output.reshape(count, query_len, heads * head_dim).astype(jnp.bfloat16)


def attend_core(query_kv, pair_qkv, pair_lengths, head_dim):
    query_len = query_kv.shape[1]
    pairs, passage_len, heads = (pair_qkv.shape[0], pair_qkv.shape[1], pair_qkv.shape[2])
    scale = head_dim ** (-0.5)
    keyset = jnp.concatenate(
        [query_kv[..., :head_dim], pair_qkv[..., head_dim : 2 * head_dim]], axis=1
    )
    values = jnp.concatenate([query_kv[..., head_dim:], pair_qkv[..., 2 * head_dim :]], axis=1)
    scores = (
        jnp.einsum(
            "bihd,bthd->bhit", pair_qkv[..., :head_dim], keyset, preferred_element_type=jnp.float32
        )
        * scale
    )
    column = jnp.arange(query_len + passage_len, dtype=jnp.int32) - query_len
    row_index = jnp.arange(passage_len, dtype=jnp.int32)
    allowed = (column[None, None, :] < 0) | (column[None, None, :] <= row_index[None, :, None]) & (
        column[None, None, :] < pair_lengths[:, None, None]
    )
    weights = softmax_rounded(scores, allowed[:, None])
    output = jnp.einsum("bhit,bthd->bihd", weights, values, preferred_element_type=jnp.float32)
    live = row_index[None, :] < pair_lengths[:, None]
    output = jnp.where(live[:, :, None, None], output, jnp.float32(0.0))
    return output.reshape(pairs, passage_len, heads * head_dim).astype(jnp.bfloat16)


def attend_pairs(query_qkv, pair_qkv, pair_lengths, head_dim, cands):
    repeated = jnp.repeat(query_qkv[..., head_dim:], cands, axis=0)
    return attend_core(repeated, pair_qkv, pair_lengths, head_dim)


def gather_store(own):
    n_store = lax.axis_size("store")
    count = own.shape[0]
    if n_store > 8 or n_store % 2:
        return lax.all_gather(own, "store", axis=0, tiled=True), lambda rows: rows
    ring = [s for s in range(0, n_store, 2)] + [s for s in range(n_store - 1, 0, -2)]
    place = [0] * n_store
    for i, s in enumerate(ring):
        place[s] = i
    forward = [(ring[i], ring[(i + 1) % n_store]) for i in range(n_store)]
    backward = [(ring[(i + 1) % n_store], ring[i]) for i in range(n_store)]
    parts = [own]
    ahead = own
    for _ in range(n_store // 2):
        ahead = lax.ppermute(ahead, "store", forward)
        parts.append(ahead)
    behind = own
    for _ in range((n_store - 1) // 2):
        behind = lax.ppermute(behind, "store", backward)
        parts.append(behind)
    place_of = jnp.asarray(place, dtype=jnp.int32)
    mine = place_of[lax.axis_index("store")]

    def rows_of(rows):
        dist = (place_of[rows // count] - mine) % n_store
        slot = jnp.where(dist == 0, 0, jnp.where(dist < n_store // 2, n_store // 2 + dist, n_store - dist))
        return slot * count + rows % count

    return jnp.concatenate(parts, axis=0), rows_of


def pair_kernel(row_query_ref, row_len_ref, pair_ref, query_ref, out_ref, *, head_dim, passage_len, query_len, chunk):
    scale = head_dim ** (-0.5)
    query_part = query_ref[0]
    query_keys = query_part[:, head_dim : 2 * head_dim]
    query_values = query_part[:, 2 * head_dim :]
    query_cols = query_keys.shape[0]
    contract = (((1,), (1,)), ((), ()))
    for start in range(0, pair_ref.shape[1], chunk):
        block = pair_ref[0, start : start + chunk, :]
        queries = block[:, :head_dim]
        keys = block[:, head_dim : 2 * head_dim]
        values = block[:, 2 * head_dim :]
        owner = row_query_ref[start : start + chunk, :]
        length = row_len_ref[start : start + chunk, :]
        to_query = lax.dot_general(queries, query_keys, contract, preferred_element_type=jnp.float32) * scale
        to_own = lax.dot_general(queries, keys, contract, preferred_element_type=jnp.float32) * scale
        query_at = lax.broadcasted_iota(jnp.int32, to_query.shape, 1) // query_len
        allow_query = query_at == owner
        row_at = lax.broadcasted_iota(jnp.int32, to_own.shape, 0)
        col_at = lax.broadcasted_iota(jnp.int32, to_own.shape, 1)
        col_tok = col_at % passage_len
        allow_own = (row_at // passage_len == col_at // passage_len) & (col_tok <= row_at % passage_len) & (col_tok < length)
        masked_query = jnp.where(allow_query, to_query, jnp.float32(-1e30))
        masked_own = jnp.where(allow_own, to_own, jnp.float32(-1e30))
        peak = jnp.maximum(jnp.max(masked_query, axis=1, keepdims=True), jnp.max(masked_own, axis=1, keepdims=True))
        exp_query = jnp.where(allow_query, jnp.exp(masked_query - peak), jnp.float32(0.0))
        exp_own = jnp.where(allow_own, jnp.exp(masked_own - peak), jnp.float32(0.0))
        total = jnp.sum(exp_query, axis=1, keepdims=True) + jnp.sum(exp_own, axis=1, keepdims=True)
        weight_query = (exp_query / total).astype(jnp.bfloat16)
        weight_own = (exp_own / total).astype(jnp.bfloat16)
        out = jnp.dot(weight_query, query_values, preferred_element_type=jnp.float32) + jnp.dot(
            weight_own, values, preferred_element_type=jnp.float32
        )
        tok = lax.broadcasted_iota(jnp.int32, out.shape, 0) % passage_len
        out_ref[0, start : start + chunk, :] = jnp.where(tok < length, out, jnp.float32(0.0)).astype(out_ref.dtype)


def attend_pairs_kernel(query_qkv, pair_qkv, pair_lengths, head_dim, cands, interpret=False):
    quer_count, query_len, heads = query_qkv.shape[0], query_qkv.shape[1], query_qkv.shape[2]
    pairs, passage_len = pair_qkv.shape[0], pair_qkv.shape[1]
    rows = pairs * passage_len
    chunk = 128 if rows % 128 == 0 and 128 % passage_len == 0 else rows
    width = 3 * head_dim
    by_head = jnp.transpose(pair_qkv, (2, 0, 1, 3)).reshape(heads, rows, width)
    query_by_head = jnp.transpose(query_qkv, (2, 0, 1, 3)).reshape(heads, quer_count * query_len, width)
    row_pair = jnp.arange(rows, dtype=jnp.int32) // passage_len
    row_query = (row_pair // cands).reshape(rows, 1)
    row_len = pair_lengths[row_pair].reshape(rows, 1)
    body = functools.partial(pair_kernel, head_dim=head_dim, passage_len=passage_len, query_len=query_len, chunk=chunk)
    out = pl.pallas_call(
        body,
        grid=(heads,),
        in_specs=[
            pl.BlockSpec((rows, 1), lambda h: (0, 0)),
            pl.BlockSpec((rows, 1), lambda h: (0, 0)),
            pl.BlockSpec((1, rows, width), lambda h: (h, 0, 0)),
            pl.BlockSpec((1, quer_count * query_len, width), lambda h: (h, 0, 0)),
        ],
        out_specs=pl.BlockSpec((1, rows, head_dim), lambda h: (h, 0, 0)),
        out_shape=jax.ShapeDtypeStruct((heads, rows, head_dim), jnp.bfloat16),
        interpret=interpret,
    )(row_query, row_len, by_head, query_by_head)
    out = jnp.transpose(out.reshape(heads, pairs, passage_len, head_dim), (1, 2, 0, 3))
    return out.reshape(pairs, passage_len, heads * head_dim)


def local(query_embeds, passage_embeds, passage_lengths, cand_passage, norm_gain, w_qkv):
    quer_count, query_len, width_part = query_embeds.shape
    pass_count, passage_len = (passage_embeds.shape[0], passage_embeds.shape[1])
    pairs_dev = cand_passage.shape[0]
    cands = pairs_dev // quer_count
    heads_part = w_qkv.shape[1]
    head_dim = w_qkv.shape[2] // 3
    query_rows = query_embeds.reshape(quer_count * query_len, width_part)
    passage_rows = passage_embeds.reshape(pass_count * passage_len, width_part)
    query_pos = jnp.tile(jnp.arange(query_len, dtype=jnp.float32), quer_count)
    passage_pos = query_len + jnp.tile(jnp.arange(passage_len, dtype=jnp.float32), pass_count)
    query_total = quer_count * query_len
    all_rows = jnp.concatenate([query_rows, passage_rows], axis=0)
    full_rows = lax.all_gather(all_rows, "tp", axis=1, tiled=True)
    normed = rms_rows(full_rows, norm_gain)
    raw = jnp.einsum("nk,khc->nhc", normed, w_qkv, preferred_element_type=jnp.float32)
    projected = rotate_parts(raw, jnp.concatenate([query_pos, passage_pos], axis=0), head_dim)
    query_qkv = projected[:query_total].reshape(quer_count, query_len, heads_part, 3 * head_dim)
    own_qkv = projected[query_total:].reshape(pass_count, passage_len, heads_part, 3 * head_dim)
    padded = jnp.arange(passage_len, dtype=jnp.int32)[None, :] >= passage_lengths[:, None]
    head_at = lax.broadcasted_iota(jnp.int32, own_qkv.shape, 2)
    col_at = lax.broadcasted_iota(jnp.int32, own_qkv.shape, 3)
    mark = padded[:, :, None, None] & (head_at == 0) & (col_at == head_dim)
    own_qkv = jnp.where(mark, jnp.asarray(jnp.inf, own_qkv.dtype), own_qkv)
    store_qkv, rows_of = gather_store(own_qkv)
    pair_qkv = store_qkv[rows_of(cand_passage)]
    pair_lengths = jnp.sum(jnp.isfinite(pair_qkv[:, :, 0, head_dim]).astype(jnp.int32), axis=1)
    query_attn = attend_queries(query_qkv, head_dim)
    passage_attn = attend_pairs_kernel(query_qkv, pair_qkv, pair_lengths, head_dim, cands)
    return (query_attn, passage_attn)


def solution(mesh):
    in_specs = (
        P("store", None, "tp"),
        P("store", None, "tp"),
        P("store"),
        P("store"),
        P(),
        P(None, "tp", None),
    )
    out_specs = (P("store", None, "tp"), P("store", None, "tp"))
    return jax.shard_map(local, mesh=mesh, in_specs=in_specs, out_specs=out_specs, check_vma=False)
```

```python
import math

import jax
import jax.numpy as jnp
from jax import lax
from jax.sharding import PartitionSpec as P


def rms_rows(rows, norm_gain):
    values = rows.astype(jnp.float32)
    meansq = jnp.mean(values * values, axis=-1, keepdims=True)
    scaled = values * lax.rsqrt(meansq + 1e-05) * norm_gain.astype(jnp.float32)
    return scaled.astype(jnp.bfloat16)


def rotate_parts(raw, positions, head_dim):
    half_dim = head_dim // 2
    inverse = jnp.exp(
        jnp.arange(half_dim, dtype=jnp.float32) * (-2.0 * math.log(10000.0) / head_dim)
    )
    angles = positions[:, None] * inverse[None, :]
    cosine = jnp.cos(angles)[:, None, :]
    sine_part = jnp.sin(angles)[:, None, :]

    def turned(block):
        first = block[..., :half_dim]
        second = block[..., half_dim:]
        return jnp.concatenate(
            [first * cosine - second * sine_part, second * cosine + first * sine_part], axis=-1
        )

    queries = turned(raw[..., :head_dim])
    keyset = turned(raw[..., head_dim : 2 * head_dim])
    values = raw[..., 2 * head_dim :]
    return jnp.concatenate([queries, keyset, values], axis=-1).astype(jnp.bfloat16)


def softmax_rounded(scores, allowed):
    masked = jnp.where(allowed, scores, jnp.float32(-1e30))
    peak = jnp.max(masked, axis=-1, keepdims=True)
    expon = jnp.where(allowed, jnp.exp(masked - peak), jnp.float32(0.0))
    return (expon / jnp.sum(expon, axis=-1, keepdims=True)).astype(jnp.bfloat16)


def attend_queries(query_qkv, head_dim):
    count, query_len, heads = (query_qkv.shape[0], query_qkv.shape[1], query_qkv.shape[2])
    scale = head_dim ** (-0.5)
    scores = (
        jnp.einsum(
            "bqhd,bkhd->bhqk",
            query_qkv[..., :head_dim],
            query_qkv[..., head_dim : 2 * head_dim],
            preferred_element_type=jnp.float32,
        )
        * scale
    )
    steps_row = jnp.arange(query_len, dtype=jnp.int32)
    allowed = steps_row[:, None] >= steps_row[None, :]
    weights = softmax_rounded(scores, allowed[None, None])
    output = jnp.einsum(
        "bhqk,bkhd->bqhd",
        weights,
        query_qkv[..., 2 * head_dim :],
        preferred_element_type=jnp.float32,
    )
    return output.reshape(count, query_len, heads * head_dim).astype(jnp.bfloat16)


def attend_core(query_kv, pair_qkv, pair_lengths, head_dim):
    query_len = query_kv.shape[1]
    pairs, passage_len, heads = (pair_qkv.shape[0], pair_qkv.shape[1], pair_qkv.shape[2])
    scale = head_dim ** (-0.5)
    keyset = jnp.concatenate(
        [query_kv[..., :head_dim], pair_qkv[..., head_dim : 2 * head_dim]], axis=1
    )
    values = jnp.concatenate([query_kv[..., head_dim:], pair_qkv[..., 2 * head_dim :]], axis=1)
    scores = (
        jnp.einsum(
            "bihd,bthd->bhit", pair_qkv[..., :head_dim], keyset, preferred_element_type=jnp.float32
        )
        * scale
    )
    column = jnp.arange(query_len + passage_len, dtype=jnp.int32) - query_len
    row_index = jnp.arange(passage_len, dtype=jnp.int32)
    allowed = (column[None, None, :] < 0) | (column[None, None, :] <= row_index[None, :, None]) & (
        column[None, None, :] < pair_lengths[:, None, None]
    )
    weights = softmax_rounded(scores, allowed[:, None])
    output = jnp.einsum("bhit,bthd->bihd", weights, values, preferred_element_type=jnp.float32)
    live = row_index[None, :] < pair_lengths[:, None]
    output = jnp.where(live[:, :, None, None], output, jnp.float32(0.0))
    return output.reshape(pairs, passage_len, heads * head_dim).astype(jnp.bfloat16)


def attend_pairs(query_qkv, pair_qkv, pair_lengths, head_dim, cands):
    repeated = jnp.repeat(query_qkv[..., head_dim:], cands, axis=0)
    return attend_core(repeated, pair_qkv, pair_lengths, head_dim)


def gather_store(own):
    n_store = lax.axis_size("store")
    count = own.shape[0]
    if n_store > 8 or n_store % 2:
        return lax.all_gather(own, "store", axis=0, tiled=True), lambda rows: rows
    ring = [s for s in range(0, n_store, 2)] + [s for s in range(n_store - 1, 0, -2)]
    place = [0] * n_store
    for i, s in enumerate(ring):
        place[s] = i
    forward = [(ring[i], ring[(i + 1) % n_store]) for i in range(n_store)]
    backward = [(ring[(i + 1) % n_store], ring[i]) for i in range(n_store)]
    steps = []
    pieces = []
    for row in range(count):
        ahead_steps = n_store // 2 if row % 2 == 0 else (n_store - 1) // 2
        behind_steps = n_store - 1 - ahead_steps
        steps.append((ahead_steps, behind_steps))
        piece = own[row : row + 1]
        parts = [piece]
        ahead = piece
        behind = piece
        for k in range(max(ahead_steps, behind_steps)):
            if k < ahead_steps:
                ahead = lax.ppermute(ahead, "store", forward)
                parts.append(ahead)
            if k < behind_steps:
                behind = lax.ppermute(behind, "store", backward)
                parts.append(behind)
        pieces.append(parts)
    ordered = []
    for row in range(count):
        ahead_steps, behind_steps = steps[row]
        parts = pieces[row]
        got_ahead, got_behind = [], []
        at = 1
        for k in range(max(ahead_steps, behind_steps)):
            if k < ahead_steps:
                got_ahead.append(parts[at])
                at += 1
            if k < behind_steps:
                got_behind.append(parts[at])
                at += 1
        ordered.extend([parts[0]] + got_ahead + got_behind)
    place_of = jnp.asarray(place, dtype=jnp.int32)
    mine = place_of[lax.axis_index("store")]
    ahead_of = jnp.asarray([s[0] for s in steps], dtype=jnp.int32)

    def rows_of(rows):
        dist = (place_of[rows // count] - mine) % n_store
        row = rows % count
        first = ahead_of[row]
        slot = jnp.where(dist == 0, 0, jnp.where(dist < n_store - first, first + dist, n_store - dist))
        return row * n_store + slot

    total = sum(part.shape[0] for part in ordered)
    row_at = lax.broadcasted_iota(jnp.int32, (total,) + own.shape[1:], 0)
    joined = None
    at = 0
    for part in ordered:
        size = part.shape[0]
        widened = jnp.pad(part, ((at, total - at - size),) + ((0, 0),) * (own.ndim - 1))
        joined = widened if joined is None else jnp.where(row_at >= at, widened, joined)
        at += size
    return joined, rows_of


def local(query_embeds, passage_embeds, passage_lengths, cand_passage, norm_gain, w_qkv):
    quer_count, query_len, width_part = query_embeds.shape
    pass_count, passage_len = (passage_embeds.shape[0], passage_embeds.shape[1])
    pairs_dev = cand_passage.shape[0]
    cands = pairs_dev // quer_count
    heads_part = w_qkv.shape[1]
    head_dim = w_qkv.shape[2] // 3
    query_rows = query_embeds.reshape(quer_count * query_len, width_part)
    passage_rows = passage_embeds.reshape(pass_count * passage_len, width_part)
    query_pos = jnp.tile(jnp.arange(query_len, dtype=jnp.float32), quer_count)
    passage_pos = query_len + jnp.tile(jnp.arange(passage_len, dtype=jnp.float32), pass_count)
    query_total = quer_count * query_len
    all_rows = jnp.concatenate([query_rows, passage_rows], axis=0)
    full_rows = lax.all_gather(all_rows, "tp", axis=1, tiled=True)
    normed = rms_rows(full_rows, norm_gain)
    raw = jnp.einsum("nk,khc->nhc", normed, w_qkv, preferred_element_type=jnp.float32)
    projected = rotate_parts(raw, jnp.concatenate([query_pos, passage_pos], axis=0), head_dim)
    query_qkv = projected[:query_total].reshape(quer_count, query_len, heads_part, 3 * head_dim)
    own_qkv = projected[query_total:].reshape(pass_count, passage_len, heads_part, 3 * head_dim)
    padded = jnp.arange(passage_len, dtype=jnp.int32)[None, :] >= passage_lengths[:, None]
    head_at = lax.broadcasted_iota(jnp.int32, own_qkv.shape, 2)
    col_at = lax.broadcasted_iota(jnp.int32, own_qkv.shape, 3)
    mark = padded[:, :, None, None] & (head_at == 0) & (col_at == head_dim)
    own_qkv = jnp.where(mark, jnp.asarray(jnp.inf, own_qkv.dtype), own_qkv)
    store_qkv, rows_of = gather_store(own_qkv)
    pair_qkv = store_qkv[rows_of(cand_passage)]
    pair_lengths = jnp.sum(jnp.isfinite(pair_qkv[:, :, 0, head_dim]).astype(jnp.int32), axis=1)
    query_attn = attend_queries(query_qkv, head_dim)
    passage_attn = attend_pairs(query_qkv, pair_qkv, pair_lengths, head_dim, cands)
    return (query_attn, passage_attn)


def solution(mesh):
    in_specs = (
        P("store", None, "tp"),
        P("store", None, "tp"),
        P("store"),
        P("store"),
        P(),
        P(None, "tp", None),
    )
    out_specs = (P("store", None, "tp"), P("store", None, "tp"))
    return jax.shard_map(local, mesh=mesh, in_specs=in_specs, out_specs=out_specs, check_vma=False)
```

```python
import math

import jax
import jax.numpy as jnp
from jax import lax
from jax.sharding import PartitionSpec as P


def rms_rows(rows, norm_gain):
    values = rows.astype(jnp.float32)
    meansq = jnp.mean(values * values, axis=-1, keepdims=True)
    scaled = values * lax.rsqrt(meansq + 1e-05) * norm_gain.astype(jnp.float32)
    return scaled.astype(jnp.bfloat16)


def rotate_parts(raw, positions, head_dim):
    half_dim = head_dim // 2
    inverse = jnp.exp(
        jnp.arange(half_dim, dtype=jnp.float32) * (-2.0 * math.log(10000.0) / head_dim)
    )
    angles = positions[:, None] * inverse[None, :]
    cosine = jnp.cos(angles)[:, None, :]
    sine_part = jnp.sin(angles)[:, None, :]

    def turned(block):
        first = block[..., :half_dim]
        second = block[..., half_dim:]
        return jnp.concatenate(
            [first * cosine - second * sine_part, second * cosine + first * sine_part], axis=-1
        )

    queries = turned(raw[..., :head_dim])
    keyset = turned(raw[..., head_dim : 2 * head_dim])
    values = raw[..., 2 * head_dim :]
    return jnp.concatenate([queries, keyset, values], axis=-1).astype(jnp.bfloat16)


def softmax_rounded(scores, allowed):
    masked = jnp.where(allowed, scores, jnp.float32(-1e30))
    peak = jnp.max(masked, axis=-1, keepdims=True)
    expon = jnp.where(allowed, jnp.exp(masked - peak), jnp.float32(0.0))
    return (expon / jnp.sum(expon, axis=-1, keepdims=True)).astype(jnp.bfloat16)


def attend_queries(query_qkv, head_dim):
    count, query_len, heads = (query_qkv.shape[0], query_qkv.shape[1], query_qkv.shape[2])
    scale = head_dim ** (-0.5)
    scores = (
        jnp.einsum(
            "bqhd,bkhd->bhqk",
            query_qkv[..., :head_dim],
            query_qkv[..., head_dim : 2 * head_dim],
            preferred_element_type=jnp.float32,
        )
        * scale
    )
    steps_row = jnp.arange(query_len, dtype=jnp.int32)
    allowed = steps_row[:, None] >= steps_row[None, :]
    weights = softmax_rounded(scores, allowed[None, None])
    output = jnp.einsum(
        "bhqk,bkhd->bqhd",
        weights,
        query_qkv[..., 2 * head_dim :],
        preferred_element_type=jnp.float32,
    )
    return output.reshape(count, query_len, heads * head_dim).astype(jnp.bfloat16)


def attend_core(query_kv, pair_qkv, pair_lengths, head_dim):
    query_len = query_kv.shape[1]
    pairs, passage_len, heads = (pair_qkv.shape[0], pair_qkv.shape[1], pair_qkv.shape[2])
    scale = head_dim ** (-0.5)
    keyset = jnp.concatenate(
        [query_kv[..., :head_dim], pair_qkv[..., head_dim : 2 * head_dim]], axis=1
    )
    values = jnp.concatenate([query_kv[..., head_dim:], pair_qkv[..., 2 * head_dim :]], axis=1)
    scores = (
        jnp.einsum(
            "bihd,bthd->bhit", pair_qkv[..., :head_dim], keyset, preferred_element_type=jnp.float32
        )
        * scale
    )
    column = jnp.arange(query_len + passage_len, dtype=jnp.int32) - query_len
    row_index = jnp.arange(passage_len, dtype=jnp.int32)
    allowed = (column[None, None, :] < 0) | (column[None, None, :] <= row_index[None, :, None]) & (
        column[None, None, :] < pair_lengths[:, None, None]
    )
    weights = softmax_rounded(scores, allowed[:, None])
    output = jnp.einsum("bhit,bthd->bihd", weights, values, preferred_element_type=jnp.float32)
    live = row_index[None, :] < pair_lengths[:, None]
    output = jnp.where(live[:, :, None, None], output, jnp.float32(0.0))
    return output.reshape(pairs, passage_len, heads * head_dim).astype(jnp.bfloat16)


def attend_pairs(query_qkv, pair_qkv, pair_lengths, head_dim, cands):
    repeated = jnp.repeat(query_qkv[..., head_dim:], cands, axis=0)
    return attend_core(repeated, pair_qkv, pair_lengths, head_dim)


def gather_store(own):
    n_store = lax.axis_size("store")
    count = own.shape[0]
    if n_store > 8 or n_store % 2:
        return lax.all_gather(own, "store", axis=0, tiled=True), lambda rows: rows
    ring = [s for s in range(0, n_store, 2)] + [s for s in range(n_store - 1, 0, -2)]
    place = [0] * n_store
    for i, s in enumerate(ring):
        place[s] = i
    forward = [(ring[i], ring[(i + 1) % n_store]) for i in range(n_store)]
    backward = [(ring[(i + 1) % n_store], ring[i]) for i in range(n_store)]
    steps = []
    pieces = []
    for row in range(count):
        ahead_steps = n_store // 2 if row % 2 == 0 else (n_store - 1) // 2
        behind_steps = n_store - 1 - ahead_steps
        steps.append((ahead_steps, behind_steps))
        piece = own[row : row + 1]
        parts = [piece]
        ahead = piece
        behind = piece
        for k in range(max(ahead_steps, behind_steps)):
            if k < ahead_steps:
                ahead = lax.ppermute(ahead, "store", forward)
                parts.append(ahead)
            if k < behind_steps:
                behind = lax.ppermute(behind, "store", backward)
                parts.append(behind)
        pieces.append(parts)
    ordered = []
    last = []
    for row in range(count):
        ahead_steps, behind_steps = steps[row]
        parts = pieces[row]
        final = max(ahead_steps, behind_steps) - 1
        got_ahead, got_behind = [], []
        at = 1
        for k in range(max(ahead_steps, behind_steps)):
            if k < ahead_steps:
                got_ahead.append((parts[at], k == final))
                at += 1
            if k < behind_steps:
                got_behind.append((parts[at], k == final))
                at += 1
        for part, is_last in [(parts[0], False)] + got_ahead + got_behind:
            ordered.append(part)
            last.append(is_last)
    place_of = jnp.asarray(place, dtype=jnp.int32)
    mine = place_of[lax.axis_index("store")]
    ahead_of = jnp.asarray([s[0] for s in steps], dtype=jnp.int32)

    def rows_of(rows):
        dist = (place_of[rows // count] - mine) % n_store
        row = rows % count
        first = ahead_of[row]
        slot = jnp.where(dist == 0, 0, jnp.where(dist < n_store - first, first + dist, n_store - dist))
        return row * n_store + slot

    total = sum(part.shape[0] for part in ordered)
    row_at = lax.broadcasted_iota(jnp.int32, (total,) + own.shape[1:], 0)
    starts = []
    at = 0
    for part in ordered:
        starts.append(at)
        at += part.shape[0]

    def lay(joined, chosen):
        for part, at in chosen:
            size = part.shape[0]
            widened = jnp.pad(part, ((at, total - at - size),) + ((0, 0),) * (own.ndim - 1))
            if joined is None:
                joined = widened
            else:
                joined = jnp.where((row_at >= at) & (row_at < at + size), widened, joined)
        return joined

    early = [(part, at) for part, at, is_last in zip(ordered, starts, last) if not is_last]
    late = [(part, at) for part, at, is_last in zip(ordered, starts, last) if is_last]
    joined = lax.optimization_barrier(lay(None, early))
    joined = lay(joined, late)
    return joined, rows_of


def local(query_embeds, passage_embeds, passage_lengths, cand_passage, norm_gain, w_qkv):
    quer_count, query_len, width_part = query_embeds.shape
    pass_count, passage_len = (passage_embeds.shape[0], passage_embeds.shape[1])
    pairs_dev = cand_passage.shape[0]
    cands = pairs_dev // quer_count
    heads_part = w_qkv.shape[1]
    head_dim = w_qkv.shape[2] // 3
    query_rows = query_embeds.reshape(quer_count * query_len, width_part)
    passage_rows = passage_embeds.reshape(pass_count * passage_len, width_part)
    query_pos = jnp.tile(jnp.arange(query_len, dtype=jnp.float32), quer_count)
    passage_pos = query_len + jnp.tile(jnp.arange(passage_len, dtype=jnp.float32), pass_count)
    query_total = quer_count * query_len
    all_rows = jnp.concatenate([query_rows, passage_rows], axis=0)
    full_rows = lax.all_gather(all_rows, "tp", axis=1, tiled=True)
    normed = rms_rows(full_rows, norm_gain)
    raw = jnp.einsum("nk,khc->nhc", normed, w_qkv, preferred_element_type=jnp.float32)
    projected = rotate_parts(raw, jnp.concatenate([query_pos, passage_pos], axis=0), head_dim)
    query_qkv = projected[:query_total].reshape(quer_count, query_len, heads_part, 3 * head_dim)
    own_qkv = projected[query_total:].reshape(pass_count, passage_len, heads_part, 3 * head_dim)
    padded = jnp.arange(passage_len, dtype=jnp.int32)[None, :] >= passage_lengths[:, None]
    head_at = lax.broadcasted_iota(jnp.int32, own_qkv.shape, 2)
    col_at = lax.broadcasted_iota(jnp.int32, own_qkv.shape, 3)
    mark = padded[:, :, None, None] & (head_at == 0) & (col_at == head_dim)
    own_qkv = jnp.where(mark, jnp.asarray(jnp.inf, own_qkv.dtype), own_qkv)
    store_qkv, rows_of = gather_store(own_qkv)
    pair_qkv = store_qkv[rows_of(cand_passage)]
    pair_lengths = jnp.sum(jnp.isfinite(pair_qkv[:, :, 0, head_dim]).astype(jnp.int32), axis=1)
    query_attn = attend_queries(query_qkv, head_dim)
    passage_attn = attend_pairs(query_qkv, pair_qkv, pair_lengths, head_dim, cands)
    return (query_attn, passage_attn)


def solution(mesh):
    in_specs = (
        P("store", None, "tp"),
        P("store", None, "tp"),
        P("store"),
        P("store"),
        P(),
        P(None, "tp", None),
    )
    out_specs = (P("store", None, "tp"), P("store", None, "tp"))
    return jax.shard_map(local, mesh=mesh, in_specs=in_specs, out_specs=out_specs, check_vma=False)
```

```python
import math

import jax
import jax.numpy as jnp
from jax import lax
from jax.sharding import PartitionSpec as P


def rms_rows(rows, norm_gain):
    values = rows.astype(jnp.float32)
    meansq = jnp.mean(values * values, axis=-1, keepdims=True)
    scaled = values * lax.rsqrt(meansq + 1e-05) * norm_gain.astype(jnp.float32)
    return scaled.astype(jnp.bfloat16)


def rotate_parts(raw, positions, head_dim):
    half_dim = head_dim // 2
    inverse = jnp.exp(
        jnp.arange(half_dim, dtype=jnp.float32) * (-2.0 * math.log(10000.0) / head_dim)
    )
    angles = positions[:, None] * inverse[None, :]
    cosine = jnp.cos(angles)[:, None, :]
    sine_part = jnp.sin(angles)[:, None, :]

    def turned(block):
        first = block[..., :half_dim]
        second = block[..., half_dim:]
        return jnp.concatenate(
            [first * cosine - second * sine_part, second * cosine + first * sine_part], axis=-1
        )

    queries = turned(raw[..., :head_dim])
    keyset = turned(raw[..., head_dim : 2 * head_dim])
    values = raw[..., 2 * head_dim :]
    return jnp.concatenate([queries, keyset, values], axis=-1).astype(jnp.bfloat16)


def softmax_rounded(scores, allowed):
    masked = jnp.where(allowed, scores, jnp.float32(-1e30))
    peak = jnp.max(masked, axis=-1, keepdims=True)
    expon = jnp.where(allowed, jnp.exp(masked - peak), jnp.float32(0.0))
    return (expon / jnp.sum(expon, axis=-1, keepdims=True)).astype(jnp.bfloat16)


def attend_queries(query_qkv, head_dim):
    count, query_len, heads = (query_qkv.shape[0], query_qkv.shape[1], query_qkv.shape[2])
    scale = head_dim ** (-0.5)
    scores = (
        jnp.einsum(
            "bqhd,bkhd->bhqk",
            query_qkv[..., :head_dim],
            query_qkv[..., head_dim : 2 * head_dim],
            preferred_element_type=jnp.float32,
        )
        * scale
    )
    steps_row = jnp.arange(query_len, dtype=jnp.int32)
    allowed = steps_row[:, None] >= steps_row[None, :]
    weights = softmax_rounded(scores, allowed[None, None])
    output = jnp.einsum(
        "bhqk,bkhd->bqhd",
        weights,
        query_qkv[..., 2 * head_dim :],
        preferred_element_type=jnp.float32,
    )
    return output.reshape(count, query_len, heads * head_dim).astype(jnp.bfloat16)


def attend_core(query_kv, pair_qkv, pair_lengths, head_dim):
    query_len = query_kv.shape[1]
    pairs, passage_len, heads = (pair_qkv.shape[0], pair_qkv.shape[1], pair_qkv.shape[2])
    scale = head_dim ** (-0.5)
    keyset = jnp.concatenate(
        [query_kv[..., :head_dim], pair_qkv[..., head_dim : 2 * head_dim]], axis=1
    )
    values = jnp.concatenate([query_kv[..., head_dim:], pair_qkv[..., 2 * head_dim :]], axis=1)
    scores = (
        jnp.einsum(
            "bihd,bthd->bhit", pair_qkv[..., :head_dim], keyset, preferred_element_type=jnp.float32
        )
        * scale
    )
    column = jnp.arange(query_len + passage_len, dtype=jnp.int32) - query_len
    row_index = jnp.arange(passage_len, dtype=jnp.int32)
    allowed = (column[None, None, :] < 0) | (column[None, None, :] <= row_index[None, :, None]) & (
        column[None, None, :] < pair_lengths[:, None, None]
    )
    weights = softmax_rounded(scores, allowed[:, None])
    output = jnp.einsum("bhit,bthd->bihd", weights, values, preferred_element_type=jnp.float32)
    live = row_index[None, :] < pair_lengths[:, None]
    output = jnp.where(live[:, :, None, None], output, jnp.float32(0.0))
    return output.reshape(pairs, passage_len, heads * head_dim).astype(jnp.bfloat16)


def attend_pairs(query_qkv, pair_qkv, pair_lengths, head_dim, cands):
    repeated = jnp.repeat(query_qkv[..., head_dim:], cands, axis=0)
    return attend_core(repeated, pair_qkv, pair_lengths, head_dim)


def gather_store(own):
    n_store = lax.axis_size("store")
    count = own.shape[0]
    if n_store > 8 or n_store % 2:
        return lax.all_gather(own, "store", axis=0, tiled=True), lambda rows: rows
    ring = [s for s in range(0, n_store, 2)] + [s for s in range(n_store - 1, 0, -2)]
    place = [0] * n_store
    for i, s in enumerate(ring):
        place[s] = i
    forward = [(ring[i], ring[(i + 1) % n_store]) for i in range(n_store)]
    backward = [(ring[(i + 1) % n_store], ring[i]) for i in range(n_store)]
    steps = []
    pieces = []
    for row in range(count):
        ahead_steps = n_store // 2 if row % 2 == 0 else (n_store - 1) // 2
        behind_steps = n_store - 1 - ahead_steps
        steps.append((ahead_steps, behind_steps))
        piece = own[row : row + 1]
        parts = [piece]
        ahead = piece
        behind = piece
        for k in range(max(ahead_steps, behind_steps)):
            if k < ahead_steps:
                ahead = lax.ppermute(ahead, "store", forward)
                parts.append(ahead)
            if k < behind_steps:
                behind = lax.ppermute(behind, "store", backward)
                parts.append(behind)
        pieces.append(parts)
    ordered = []
    arrival = []
    for row in range(count):
        ahead_steps, behind_steps = steps[row]
        parts = pieces[row]
        got_ahead, got_behind = [], []
        at = 1
        for k in range(max(ahead_steps, behind_steps)):
            if k < ahead_steps:
                got_ahead.append((parts[at], k + 1))
                at += 1
            if k < behind_steps:
                got_behind.append((parts[at], k + 1))
                at += 1
        for part, step in [(parts[0], 0)] + got_ahead + got_behind:
            ordered.append(part)
            arrival.append(step)
    place_of = jnp.asarray(place, dtype=jnp.int32)
    mine = place_of[lax.axis_index("store")]
    ahead_of = jnp.asarray([s[0] for s in steps], dtype=jnp.int32)

    def rows_of(rows):
        dist = (place_of[rows // count] - mine) % n_store
        row = rows % count
        first = ahead_of[row]
        slot = jnp.where(dist == 0, 0, jnp.where(dist < n_store - first, first + dist, n_store - dist))
        return row * n_store + slot

    total = sum(part.shape[0] for part in ordered)
    row_at = lax.broadcasted_iota(jnp.int32, (total,) + own.shape[1:], 0)
    starts = []
    at = 0
    for part in ordered:
        starts.append(at)
        at += part.shape[0]

    def lay(joined, chosen):
        for part, at in chosen:
            size = part.shape[0]
            widened = jnp.pad(part, ((at, total - at - size),) + ((0, 0),) * (own.ndim - 1))
            if joined is None:
                joined = widened
            else:
                joined = jnp.where((row_at >= at) & (row_at < at + size), widened, joined)
        return joined

    last_step = max(arrival)
    first_join = max(last_step - 2, 0)
    joined = lay(None, [(p, a) for p, a, s in zip(ordered, starts, arrival) if s <= first_join])
    for step in range(first_join + 1, last_step + 1):
        joined = lax.optimization_barrier(joined)
        joined = lay(joined, [(p, a) for p, a, s in zip(ordered, starts, arrival) if s == step])
    return joined, rows_of


def local(query_embeds, passage_embeds, passage_lengths, cand_passage, norm_gain, w_qkv):
    quer_count, query_len, width_part = query_embeds.shape
    pass_count, passage_len = (passage_embeds.shape[0], passage_embeds.shape[1])
    pairs_dev = cand_passage.shape[0]
    cands = pairs_dev // quer_count
    heads_part = w_qkv.shape[1]
    head_dim = w_qkv.shape[2] // 3
    query_rows = query_embeds.reshape(quer_count * query_len, width_part)
    passage_rows = passage_embeds.reshape(pass_count * passage_len, width_part)
    query_pos = jnp.tile(jnp.arange(query_len, dtype=jnp.float32), quer_count)
    passage_pos = query_len + jnp.tile(jnp.arange(passage_len, dtype=jnp.float32), pass_count)
    query_total = quer_count * query_len
    all_rows = jnp.concatenate([query_rows, passage_rows], axis=0)
    full_rows = lax.all_gather(all_rows, "tp", axis=1, tiled=True)
    normed = rms_rows(full_rows, norm_gain)
    raw = jnp.einsum("nk,khc->nhc", normed, w_qkv, preferred_element_type=jnp.float32)
    projected = rotate_parts(raw, jnp.concatenate([query_pos, passage_pos], axis=0), head_dim)
    query_qkv = projected[:query_total].reshape(quer_count, query_len, heads_part, 3 * head_dim)
    own_qkv = projected[query_total:].reshape(pass_count, passage_len, heads_part, 3 * head_dim)
    padded = jnp.arange(passage_len, dtype=jnp.int32)[None, :] >= passage_lengths[:, None]
    head_at = lax.broadcasted_iota(jnp.int32, own_qkv.shape, 2)
    col_at = lax.broadcasted_iota(jnp.int32, own_qkv.shape, 3)
    mark = padded[:, :, None, None] & (head_at == 0) & (col_at == head_dim)
    own_qkv = jnp.where(mark, jnp.asarray(jnp.inf, own_qkv.dtype), own_qkv)
    store_qkv, rows_of = gather_store(own_qkv)
    pair_qkv = store_qkv[rows_of(cand_passage)]
    pair_lengths = jnp.sum(jnp.isfinite(pair_qkv[:, :, 0, head_dim]).astype(jnp.int32), axis=1)
    query_attn = attend_queries(query_qkv, head_dim)
    passage_attn = attend_pairs(query_qkv, pair_qkv, pair_lengths, head_dim, cands)
    return (query_attn, passage_attn)


def solution(mesh):
    in_specs = (
        P("store", None, "tp"),
        P("store", None, "tp"),
        P("store"),
        P("store"),
        P(),
        P(None, "tp", None),
    )
    out_specs = (P("store", None, "tp"), P("store", None, "tp"))
    return jax.shard_map(local, mesh=mesh, in_specs=in_specs, out_specs=out_specs, check_vma=False)
```

```python
import math

import jax
import jax.numpy as jnp
from jax import lax
from jax.sharding import PartitionSpec as P


def rms_rows(rows, norm_gain):
    values = rows.astype(jnp.float32)
    meansq = jnp.mean(values * values, axis=-1, keepdims=True)
    scaled = values * lax.rsqrt(meansq + 1e-05) * norm_gain.astype(jnp.float32)
    return scaled.astype(jnp.bfloat16)


def rotate_parts(raw, positions, head_dim):
    half_dim = head_dim // 2
    inverse = jnp.exp(
        jnp.arange(half_dim, dtype=jnp.float32) * (-2.0 * math.log(10000.0) / head_dim)
    )
    angles = positions[:, None] * inverse[None, :]
    cosine = jnp.cos(angles)[:, None, :]
    sine_part = jnp.sin(angles)[:, None, :]

    def turned(block):
        first = block[..., :half_dim]
        second = block[..., half_dim:]
        return jnp.concatenate(
            [first * cosine - second * sine_part, second * cosine + first * sine_part], axis=-1
        )

    queries = turned(raw[..., :head_dim])
    keyset = turned(raw[..., head_dim : 2 * head_dim])
    values = raw[..., 2 * head_dim :]
    return jnp.concatenate([queries, keyset, values], axis=-1).astype(jnp.bfloat16)


def softmax_rounded(scores, allowed):
    masked = jnp.where(allowed, scores, jnp.float32(-1e30))
    peak = jnp.max(masked, axis=-1, keepdims=True)
    expon = jnp.where(allowed, jnp.exp(masked - peak), jnp.float32(0.0))
    return (expon / jnp.sum(expon, axis=-1, keepdims=True)).astype(jnp.bfloat16)


def attend_queries(query_qkv, head_dim):
    count, query_len, heads = (query_qkv.shape[0], query_qkv.shape[1], query_qkv.shape[2])
    scale = head_dim ** (-0.5)
    scores = (
        jnp.einsum(
            "bqhd,bkhd->bhqk",
            query_qkv[..., :head_dim],
            query_qkv[..., head_dim : 2 * head_dim],
            preferred_element_type=jnp.float32,
        )
        * scale
    )
    steps_row = jnp.arange(query_len, dtype=jnp.int32)
    allowed = steps_row[:, None] >= steps_row[None, :]
    weights = softmax_rounded(scores, allowed[None, None])
    output = jnp.einsum(
        "bhqk,bkhd->bqhd",
        weights,
        query_qkv[..., 2 * head_dim :],
        preferred_element_type=jnp.float32,
    )
    return output.reshape(count, query_len, heads * head_dim).astype(jnp.bfloat16)


def attend_core(query_kv, pair_qkv, head_dim):
    query_len = query_kv.shape[1]
    pairs, passage_len, heads = (pair_qkv.shape[0], pair_qkv.shape[1], pair_qkv.shape[2])
    scale = head_dim ** (-0.5)
    keyset = jnp.concatenate(
        [query_kv[..., :head_dim], pair_qkv[..., head_dim : 2 * head_dim]], axis=1
    )
    values = jnp.concatenate([query_kv[..., head_dim:], pair_qkv[..., 2 * head_dim :]], axis=1)
    scores = (
        jnp.einsum(
            "bihd,bthd->bhit", pair_qkv[..., :head_dim], keyset, preferred_element_type=jnp.float32
        )
        * scale
    )
    column = jnp.arange(query_len + passage_len, dtype=jnp.int32) - query_len
    row_index = jnp.arange(passage_len, dtype=jnp.int32)
    present = jnp.isfinite(pair_qkv[:, :, 0, head_dim])
    present_cols = jnp.concatenate([jnp.ones((pairs, query_len), jnp.bool_), present], axis=1)
    allowed = (column[None, None, :] < 0) | (column[None, None, :] <= row_index[None, :, None]) & present_cols[:, None, :]
    weights = softmax_rounded(scores, allowed[:, None])
    output = jnp.einsum("bhit,bthd->bihd", weights, values, preferred_element_type=jnp.float32)
    live = present
    output = jnp.where(live[:, :, None, None], output, jnp.float32(0.0))
    return output.reshape(pairs, passage_len, heads * head_dim).astype(jnp.bfloat16)


def attend_pairs(query_qkv, pair_qkv, head_dim, cands):
    repeated = jnp.repeat(query_qkv[..., head_dim:], cands, axis=0)
    return attend_core(repeated, pair_qkv, head_dim)


def gather_store(own):
    n_store = lax.axis_size("store")
    count = own.shape[0]
    if n_store > 8 or n_store % 2:
        return lax.all_gather(own, "store", axis=0, tiled=True), lambda rows: rows
    ring = [s for s in range(0, n_store, 2)] + [s for s in range(n_store - 1, 0, -2)]
    place = [0] * n_store
    for i, s in enumerate(ring):
        place[s] = i
    forward = [(ring[i], ring[(i + 1) % n_store]) for i in range(n_store)]
    backward = [(ring[(i + 1) % n_store], ring[i]) for i in range(n_store)]
    steps = []
    pieces = []
    for row in range(count):
        ahead_steps = n_store // 2 if row % 2 == 0 else (n_store - 1) // 2
        behind_steps = n_store - 1 - ahead_steps
        steps.append((ahead_steps, behind_steps))
        piece = own[row : row + 1]
        parts = [piece]
        ahead = piece
        behind = piece
        for k in range(max(ahead_steps, behind_steps)):
            if k < ahead_steps:
                ahead = lax.ppermute(ahead, "store", forward)
                parts.append(ahead)
            if k < behind_steps:
                behind = lax.ppermute(behind, "store", backward)
                parts.append(behind)
        pieces.append(parts)
    ordered = []
    arrival = []
    for row in range(count):
        ahead_steps, behind_steps = steps[row]
        parts = pieces[row]
        got_ahead, got_behind = [], []
        at = 1
        for k in range(max(ahead_steps, behind_steps)):
            if k < ahead_steps:
                got_ahead.append((parts[at], k + 1))
                at += 1
            if k < behind_steps:
                got_behind.append((parts[at], k + 1))
                at += 1
        for part, step in [(parts[0], 0)] + got_ahead + got_behind:
            ordered.append(part)
            arrival.append(step)
    place_of = jnp.asarray(place, dtype=jnp.int32)
    mine = place_of[lax.axis_index("store")]
    ahead_of = jnp.asarray([s[0] for s in steps], dtype=jnp.int32)

    def rows_of(rows):
        dist = (place_of[rows // count] - mine) % n_store
        row = rows % count
        first = ahead_of[row]
        slot = jnp.where(dist == 0, 0, jnp.where(dist < n_store - first, first + dist, n_store - dist))
        return row * n_store + slot

    total = sum(part.shape[0] for part in ordered)
    row_at = lax.broadcasted_iota(jnp.int32, (total,) + own.shape[1:], 0)
    starts = []
    at = 0
    for part in ordered:
        starts.append(at)
        at += part.shape[0]

    def lay(joined, chosen):
        for part, at in chosen:
            size = part.shape[0]
            widened = jnp.pad(part, ((at, total - at - size),) + ((0, 0),) * (own.ndim - 1))
            if joined is None:
                joined = widened
            else:
                joined = jnp.where((row_at >= at) & (row_at < at + size), widened, joined)
        return joined

    last_step = max(arrival)
    first_join = max(last_step - 2, 0)
    joined = lay(None, [(p, a) for p, a, s in zip(ordered, starts, arrival) if s <= first_join])
    for step in range(first_join + 1, last_step + 1):
        joined = lax.optimization_barrier(joined)
        joined = lay(joined, [(p, a) for p, a, s in zip(ordered, starts, arrival) if s == step])
    return joined, rows_of


def local(query_embeds, passage_embeds, passage_lengths, cand_passage, norm_gain, w_qkv):
    quer_count, query_len, width_part = query_embeds.shape
    pass_count, passage_len = (passage_embeds.shape[0], passage_embeds.shape[1])
    pairs_dev = cand_passage.shape[0]
    cands = pairs_dev // quer_count
    heads_part = w_qkv.shape[1]
    head_dim = w_qkv.shape[2] // 3
    query_rows = query_embeds.reshape(quer_count * query_len, width_part)
    passage_rows = passage_embeds.reshape(pass_count * passage_len, width_part)
    query_pos = jnp.tile(jnp.arange(query_len, dtype=jnp.float32), quer_count)
    passage_pos = query_len + jnp.tile(jnp.arange(passage_len, dtype=jnp.float32), pass_count)
    query_total = quer_count * query_len
    all_rows = jnp.concatenate([query_rows, passage_rows], axis=0)
    full_rows = lax.all_gather(all_rows, "tp", axis=1, tiled=True)
    normed = rms_rows(full_rows, norm_gain)
    raw = jnp.einsum("nk,khc->nhc", normed, w_qkv, preferred_element_type=jnp.float32)
    projected = rotate_parts(raw, jnp.concatenate([query_pos, passage_pos], axis=0), head_dim)
    query_qkv = projected[:query_total].reshape(quer_count, query_len, heads_part, 3 * head_dim)
    own_qkv = projected[query_total:].reshape(pass_count, passage_len, heads_part, 3 * head_dim)
    padded = jnp.arange(passage_len, dtype=jnp.int32)[None, :] >= passage_lengths[:, None]
    head_at = lax.broadcasted_iota(jnp.int32, own_qkv.shape, 2)
    col_at = lax.broadcasted_iota(jnp.int32, own_qkv.shape, 3)
    mark = padded[:, :, None, None] & (head_at == 0) & (col_at == head_dim)
    own_qkv = jnp.where(mark, jnp.asarray(jnp.inf, own_qkv.dtype), own_qkv)
    store_qkv, rows_of = gather_store(own_qkv)
    pair_qkv = store_qkv[rows_of(cand_passage)]
    query_attn = attend_queries(query_qkv, head_dim)
    passage_attn = attend_pairs(query_qkv, pair_qkv, head_dim, cands)
    return (query_attn, passage_attn)


def solution(mesh):
    in_specs = (
        P("store", None, "tp"),
        P("store", None, "tp"),
        P("store"),
        P("store"),
        P(),
        P(None, "tp", None),
    )
    out_specs = (P("store", None, "tp"), P("store", None, "tp"))
    return jax.shard_map(local, mesh=mesh, in_specs=in_specs, out_specs=out_specs, check_vma=False)
```

```python
import math

import jax
import jax.numpy as jnp
from jax import lax
from jax.sharding import PartitionSpec as P


def rms_rows(rows, norm_gain):
    values = rows.astype(jnp.float32)
    meansq = jnp.mean(values * values, axis=-1, keepdims=True)
    scaled = values * lax.rsqrt(meansq + 1e-05) * norm_gain.astype(jnp.float32)
    return scaled.astype(jnp.bfloat16)


def rotate_parts(raw, positions, head_dim):
    half_dim = head_dim // 2
    inverse = jnp.exp(
        jnp.arange(half_dim, dtype=jnp.float32) * (-2.0 * math.log(10000.0) / head_dim)
    )
    angles = positions[:, None] * inverse[None, :]
    cosine = jnp.cos(angles)[:, None, :]
    sine_part = jnp.sin(angles)[:, None, :]

    def turned(block):
        first = block[..., :half_dim]
        second = block[..., half_dim:]
        return jnp.concatenate(
            [first * cosine - second * sine_part, second * cosine + first * sine_part], axis=-1
        )

    queries = turned(raw[..., :head_dim])
    keyset = turned(raw[..., head_dim : 2 * head_dim])
    values = raw[..., 2 * head_dim :]
    return jnp.concatenate([queries, keyset, values], axis=-1).astype(jnp.bfloat16)


def softmax_rounded(scores, allowed):
    masked = jnp.where(allowed, scores, jnp.float32(-1e30))
    peak = jnp.max(masked, axis=-1, keepdims=True)
    expon = jnp.where(allowed, jnp.exp(masked - peak), jnp.float32(0.0))
    return (expon / jnp.sum(expon, axis=-1, keepdims=True)).astype(jnp.bfloat16)


def attend_queries(query_qkv, head_dim):
    count, query_len, heads = (query_qkv.shape[0], query_qkv.shape[1], query_qkv.shape[2])
    scale = head_dim ** (-0.5)
    scores = (
        jnp.einsum(
            "bqhd,bkhd->bhqk",
            query_qkv[..., :head_dim],
            query_qkv[..., head_dim : 2 * head_dim],
            preferred_element_type=jnp.float32,
        )
        * scale
    )
    steps_row = jnp.arange(query_len, dtype=jnp.int32)
    allowed = steps_row[:, None] >= steps_row[None, :]
    weights = softmax_rounded(scores, allowed[None, None])
    output = jnp.einsum(
        "bhqk,bkhd->bqhd",
        weights,
        query_qkv[..., 2 * head_dim :],
        preferred_element_type=jnp.float32,
    )
    return output.reshape(count, query_len, heads * head_dim).astype(jnp.bfloat16)


def attend_core(query_kv, pair_q, pair_k, pair_v, pair_lengths, head_dim):
    query_len = query_kv.shape[1]
    pairs, passage_len, heads = (pair_q.shape[0], pair_q.shape[1], pair_q.shape[2])
    scale = head_dim ** (-0.5)
    keyset = jnp.concatenate(
        [query_kv[..., :head_dim], pair_k], axis=1
    )
    values = jnp.concatenate([query_kv[..., head_dim:], pair_v], axis=1)
    scores = (
        jnp.einsum(
            "bihd,bthd->bhit", pair_q, keyset, preferred_element_type=jnp.float32
        )
        * scale
    )
    column = jnp.arange(query_len + passage_len, dtype=jnp.int32) - query_len
    row_index = jnp.arange(passage_len, dtype=jnp.int32)
    allowed = (column[None, None, :] < 0) | (column[None, None, :] <= row_index[None, :, None]) & (
        column[None, None, :] < pair_lengths[:, None, None]
    )
    weights = softmax_rounded(scores, allowed[:, None])
    output = jnp.einsum("bhit,bthd->bihd", weights, values, preferred_element_type=jnp.float32)
    live = row_index[None, :] < pair_lengths[:, None]
    output = jnp.where(live[:, :, None, None], output, jnp.float32(0.0))
    return output.reshape(pairs, passage_len, heads * head_dim).astype(jnp.bfloat16)


def attend_pairs(query_qkv, pair_q, pair_k, pair_v, pair_lengths, head_dim, cands):
    repeated = jnp.repeat(query_qkv[..., head_dim:], cands, axis=0)
    return attend_core(repeated, pair_q, pair_k, pair_v, pair_lengths, head_dim)


def gather_store(own):
    n_store = lax.axis_size("store")
    count = own.shape[0]
    if n_store > 8 or n_store % 2:
        return lax.all_gather(own, "store", axis=0, tiled=True), lambda rows: rows
    ring = [s for s in range(0, n_store, 2)] + [s for s in range(n_store - 1, 0, -2)]
    place = [0] * n_store
    for i, s in enumerate(ring):
        place[s] = i
    forward = [(ring[i], ring[(i + 1) % n_store]) for i in range(n_store)]
    backward = [(ring[(i + 1) % n_store], ring[i]) for i in range(n_store)]
    steps = []
    pieces = []
    for row in range(count):
        ahead_steps = n_store // 2 if row % 2 == 0 else (n_store - 1) // 2
        behind_steps = n_store - 1 - ahead_steps
        steps.append((ahead_steps, behind_steps))
        piece = own[row : row + 1]
        parts = [piece]
        ahead = piece
        behind = piece
        for k in range(max(ahead_steps, behind_steps)):
            if k < ahead_steps:
                ahead = lax.ppermute(ahead, "store", forward)
                parts.append(ahead)
            if k < behind_steps:
                behind = lax.ppermute(behind, "store", backward)
                parts.append(behind)
        pieces.append(parts)
    ordered = []
    arrival = []
    for row in range(count):
        ahead_steps, behind_steps = steps[row]
        parts = pieces[row]
        got_ahead, got_behind = [], []
        at = 1
        for k in range(max(ahead_steps, behind_steps)):
            if k < ahead_steps:
                got_ahead.append((parts[at], k + 1))
                at += 1
            if k < behind_steps:
                got_behind.append((parts[at], k + 1))
                at += 1
        for part, step in [(parts[0], 0)] + got_ahead + got_behind:
            ordered.append(part)
            arrival.append(step)
    place_of = jnp.asarray(place, dtype=jnp.int32)
    mine = place_of[lax.axis_index("store")]
    ahead_of = jnp.asarray([s[0] for s in steps], dtype=jnp.int32)

    def rows_of(rows):
        dist = (place_of[rows // count] - mine) % n_store
        row = rows % count
        first = ahead_of[row]
        slot = jnp.where(dist == 0, 0, jnp.where(dist < n_store - first, first + dist, n_store - dist))
        return row * n_store + slot

    total = sum(part.shape[0] for part in ordered)
    row_at = lax.broadcasted_iota(jnp.int32, (total,) + own.shape[1:], 0)
    starts = []
    at = 0
    for part in ordered:
        starts.append(at)
        at += part.shape[0]

    def lay(joined, chosen):
        for part, at in chosen:
            size = part.shape[0]
            widened = jnp.pad(part, ((at, total - at - size),) + ((0, 0),) * (own.ndim - 1))
            if joined is None:
                joined = widened
            else:
                joined = jnp.where((row_at >= at) & (row_at < at + size), widened, joined)
        return joined

    last_step = max(arrival)
    first_join = max(last_step - 2, 0)
    joined = lay(None, [(p, a) for p, a, s in zip(ordered, starts, arrival) if s <= first_join])
    for step in range(first_join + 1, last_step + 1):
        joined = lax.optimization_barrier(joined)
        joined = lay(joined, [(p, a) for p, a, s in zip(ordered, starts, arrival) if s == step])
    return joined, rows_of


def local(query_embeds, passage_embeds, passage_lengths, cand_passage, norm_gain, w_qkv):
    quer_count, query_len, width_part = query_embeds.shape
    pass_count, passage_len = (passage_embeds.shape[0], passage_embeds.shape[1])
    pairs_dev = cand_passage.shape[0]
    cands = pairs_dev // quer_count
    heads_part = w_qkv.shape[1]
    head_dim = w_qkv.shape[2] // 3
    query_rows = query_embeds.reshape(quer_count * query_len, width_part)
    passage_rows = passage_embeds.reshape(pass_count * passage_len, width_part)
    query_pos = jnp.tile(jnp.arange(query_len, dtype=jnp.float32), quer_count)
    passage_pos = query_len + jnp.tile(jnp.arange(passage_len, dtype=jnp.float32), pass_count)
    query_total = quer_count * query_len
    all_rows = jnp.concatenate([query_rows, passage_rows], axis=0)
    full_rows = lax.all_gather(all_rows, "tp", axis=1, tiled=True)
    normed = rms_rows(full_rows, norm_gain)
    raw = jnp.einsum("nk,khc->nhc", normed, w_qkv, preferred_element_type=jnp.float32)
    projected = rotate_parts(raw, jnp.concatenate([query_pos, passage_pos], axis=0), head_dim)
    query_qkv = projected[:query_total].reshape(quer_count, query_len, heads_part, 3 * head_dim)
    own_qkv = projected[query_total:].reshape(pass_count, passage_len, heads_part, 3 * head_dim)
    padded = jnp.arange(passage_len, dtype=jnp.int32)[None, :] >= passage_lengths[:, None]
    head_at = lax.broadcasted_iota(jnp.int32, own_qkv.shape, 2)
    col_at = lax.broadcasted_iota(jnp.int32, own_qkv.shape, 3)
    mark = padded[:, :, None, None] & (head_at == 0) & (col_at == head_dim)
    own_qkv = jnp.where(mark, jnp.asarray(jnp.inf, own_qkv.dtype), own_qkv)
    store_qkv, rows_of = gather_store(own_qkv)
    rows = rows_of(cand_passage)
    pair_q = store_qkv[:, :, :, :head_dim][rows]
    pair_k = store_qkv[:, :, :, head_dim : 2 * head_dim][rows]
    pair_v = store_qkv[:, :, :, 2 * head_dim :][rows]
    pair_lengths = jnp.sum(jnp.isfinite(pair_k[:, :, 0, 0]).astype(jnp.int32), axis=1)
    query_attn = attend_queries(query_qkv, head_dim)
    passage_attn = attend_pairs(query_qkv, pair_q, pair_k, pair_v, pair_lengths, head_dim, cands)
    return (query_attn, passage_attn)


def solution(mesh):
    in_specs = (
        P("store", None, "tp"),
        P("store", None, "tp"),
        P("store"),
        P("store"),
        P(),
        P(None, "tp", None),
    )
    out_specs = (P("store", None, "tp"), P("store", None, "tp"))
    return jax.shard_map(local, mesh=mesh, in_specs=in_specs, out_specs=out_specs, check_vma=False)
```

```python
import math

import jax
import jax.numpy as jnp
from jax import lax
from jax.sharding import PartitionSpec as P


def rms_rows(rows, norm_gain):
    values = rows.astype(jnp.float32)
    meansq = jnp.mean(values * values, axis=-1, keepdims=True)
    scaled = values * lax.rsqrt(meansq + 1e-05) * norm_gain.astype(jnp.float32)
    return scaled.astype(jnp.bfloat16)


def rotate_parts(raw, positions, head_dim):
    half_dim = head_dim // 2
    inverse = jnp.exp(
        jnp.arange(half_dim, dtype=jnp.float32) * (-2.0 * math.log(10000.0) / head_dim)
    )
    angles = positions[:, None] * inverse[None, :]
    cosine = jnp.cos(angles)[:, None, :]
    sine_part = jnp.sin(angles)[:, None, :]

    def turned(block):
        first = block[..., :half_dim]
        second = block[..., half_dim:]
        return jnp.concatenate(
            [first * cosine - second * sine_part, second * cosine + first * sine_part], axis=-1
        )

    queries = turned(raw[..., :head_dim])
    keyset = turned(raw[..., head_dim : 2 * head_dim])
    values = raw[..., 2 * head_dim :]
    return jnp.concatenate([queries, keyset, values], axis=-1).astype(jnp.bfloat16)


def softmax_rounded(scores, allowed):
    masked = jnp.where(allowed, scores, jnp.float32(-1e30))
    peak = jnp.max(masked, axis=-1, keepdims=True)
    expon = jnp.where(allowed, jnp.exp(masked - peak), jnp.float32(0.0))
    return (expon / jnp.sum(expon, axis=-1, keepdims=True)).astype(jnp.bfloat16)


def attend_queries(query_qkv, head_dim):
    count, query_len, heads = (query_qkv.shape[0], query_qkv.shape[1], query_qkv.shape[2])
    scale = head_dim ** (-0.5)
    scores = (
        jnp.einsum(
            "bqhd,bkhd->bhqk",
            query_qkv[..., :head_dim],
            query_qkv[..., head_dim : 2 * head_dim],
            preferred_element_type=jnp.float32,
        )
        * scale
    )
    steps_row = jnp.arange(query_len, dtype=jnp.int32)
    allowed = steps_row[:, None] >= steps_row[None, :]
    weights = softmax_rounded(scores, allowed[None, None])
    output = jnp.einsum(
        "bhqk,bkhd->bqhd",
        weights,
        query_qkv[..., 2 * head_dim :],
        preferred_element_type=jnp.float32,
    )
    return output.reshape(count, query_len, heads * head_dim).astype(jnp.bfloat16)


def attend_core(query_kv, pair_q, pair_k, pair_v, pair_lengths, head_dim):
    query_len = query_kv.shape[1]
    pairs, passage_len, heads = (pair_q.shape[0], pair_q.shape[1], pair_q.shape[2])
    scale = head_dim ** (-0.5)
    keyset = jnp.concatenate(
        [query_kv[..., :head_dim], pair_k], axis=1
    )
    values = jnp.concatenate([query_kv[..., head_dim:], pair_v], axis=1)
    scores = (
        jnp.einsum(
            "bihd,bthd->bhit", pair_q, keyset, preferred_element_type=jnp.float32
        )
        * scale
    )
    column = jnp.arange(query_len + passage_len, dtype=jnp.int32) - query_len
    row_index = jnp.arange(passage_len, dtype=jnp.int32)
    allowed = (column[None, None, :] < 0) | (column[None, None, :] <= row_index[None, :, None]) & (
        column[None, None, :] < pair_lengths[:, None, None]
    )
    weights = softmax_rounded(scores, allowed[:, None])
    output = jnp.einsum("bhit,bthd->bihd", weights, values, preferred_element_type=jnp.float32)
    live = row_index[None, :] < pair_lengths[:, None]
    output = jnp.where(live[:, :, None, None], output, jnp.float32(0.0))
    return output.reshape(pairs, passage_len, heads * head_dim).astype(jnp.bfloat16)


def attend_pairs(query_qkv, pair_q, pair_k, pair_v, pair_lengths, head_dim, cands):
    repeated = jnp.repeat(query_qkv[..., head_dim:], cands, axis=0)
    return attend_core(repeated, pair_q, pair_k, pair_v, pair_lengths, head_dim)


def gather_store(own):
    n_store = lax.axis_size("store")
    count = own.shape[0]
    if n_store > 8 or n_store % 2:
        return lax.all_gather(own, "store", axis=0, tiled=True), lambda rows: rows
    ring = [s for s in range(0, n_store, 2)] + [s for s in range(n_store - 1, 0, -2)]
    place = [0] * n_store
    for i, s in enumerate(ring):
        place[s] = i
    forward = [(ring[i], ring[(i + 1) % n_store]) for i in range(n_store)]
    backward = [(ring[(i + 1) % n_store], ring[i]) for i in range(n_store)]
    steps = []
    pieces = []
    for row in range(count):
        ahead_steps = n_store // 2 if row % 2 == 0 else (n_store - 1) // 2
        behind_steps = n_store - 1 - ahead_steps
        steps.append((ahead_steps, behind_steps))
        piece = own[row : row + 1]
        parts = [piece]
        ahead = piece
        behind = piece
        for k in range(max(ahead_steps, behind_steps)):
            if k < ahead_steps:
                ahead = lax.ppermute(ahead, "store", forward)
                parts.append(ahead)
            if k < behind_steps:
                behind = lax.ppermute(behind, "store", backward)
                parts.append(behind)
        pieces.append(parts)
    ordered = []
    arrival = []
    for row in range(count):
        ahead_steps, behind_steps = steps[row]
        parts = pieces[row]
        got_ahead, got_behind = [], []
        at = 1
        for k in range(max(ahead_steps, behind_steps)):
            if k < ahead_steps:
                got_ahead.append((parts[at], k + 1))
                at += 1
            if k < behind_steps:
                got_behind.append((parts[at], k + 1))
                at += 1
        for part, step in [(parts[0], 0)] + got_ahead + got_behind:
            ordered.append(part)
            arrival.append(step)
    place_of = jnp.asarray(place, dtype=jnp.int32)
    mine = place_of[lax.axis_index("store")]
    ahead_of = jnp.asarray([s[0] for s in steps], dtype=jnp.int32)

    def rows_of(rows):
        dist = (place_of[rows // count] - mine) % n_store
        row = rows % count
        first = ahead_of[row]
        slot = jnp.where(dist == 0, 0, jnp.where(dist < n_store - first, first + dist, n_store - dist))
        return row * n_store + slot

    total = sum(part.shape[0] for part in ordered)
    row_at = lax.broadcasted_iota(jnp.int32, (total,) + own.shape[1:], 0)
    starts = []
    at = 0
    for part in ordered:
        starts.append(at)
        at += part.shape[0]

    def lay(joined, chosen):
        for part, at in chosen:
            size = part.shape[0]
            widened = jnp.pad(part, ((at, total - at - size),) + ((0, 0),) * (own.ndim - 1))
            if joined is None:
                joined = widened
            else:
                joined = jnp.where((row_at >= at) & (row_at < at + size), widened, joined)
        return joined

    last_step = max(arrival)
    first_join = min(1, last_step)
    joined = lay(None, [(p, a) for p, a, s in zip(ordered, starts, arrival) if s <= first_join])
    for step in range(first_join + 1, last_step + 1):
        joined = lax.optimization_barrier(joined)
        joined = lay(joined, [(p, a) for p, a, s in zip(ordered, starts, arrival) if s == step])
    return joined, rows_of


def local(query_embeds, passage_embeds, passage_lengths, cand_passage, norm_gain, w_qkv):
    quer_count, query_len, width_part = query_embeds.shape
    pass_count, passage_len = (passage_embeds.shape[0], passage_embeds.shape[1])
    pairs_dev = cand_passage.shape[0]
    cands = pairs_dev // quer_count
    heads_part = w_qkv.shape[1]
    head_dim = w_qkv.shape[2] // 3
    query_rows = query_embeds.reshape(quer_count * query_len, width_part)
    passage_rows = passage_embeds.reshape(pass_count * passage_len, width_part)
    query_pos = jnp.tile(jnp.arange(query_len, dtype=jnp.float32), quer_count)
    passage_pos = query_len + jnp.tile(jnp.arange(passage_len, dtype=jnp.float32), pass_count)
    query_total = quer_count * query_len
    all_rows = jnp.concatenate([query_rows, passage_rows], axis=0)
    full_rows = lax.all_gather(all_rows, "tp", axis=1, tiled=True)
    normed = rms_rows(full_rows, norm_gain)
    raw = jnp.einsum("nk,khc->nhc", normed, w_qkv, preferred_element_type=jnp.float32)
    projected = rotate_parts(raw, jnp.concatenate([query_pos, passage_pos], axis=0), head_dim)
    query_qkv = projected[:query_total].reshape(quer_count, query_len, heads_part, 3 * head_dim)
    own_qkv = projected[query_total:].reshape(pass_count, passage_len, heads_part, 3 * head_dim)
    padded = jnp.arange(passage_len, dtype=jnp.int32)[None, :] >= passage_lengths[:, None]
    head_at = lax.broadcasted_iota(jnp.int32, own_qkv.shape, 2)
    col_at = lax.broadcasted_iota(jnp.int32, own_qkv.shape, 3)
    mark = padded[:, :, None, None] & (head_at == 0) & (col_at == head_dim)
    own_qkv = jnp.where(mark, jnp.asarray(jnp.inf, own_qkv.dtype), own_qkv)
    store_qkv, rows_of = gather_store(own_qkv)
    rows = rows_of(cand_passage)
    pair_q = store_qkv[:, :, :, :head_dim][rows]
    pair_k = store_qkv[:, :, :, head_dim : 2 * head_dim][rows]
    pair_v = store_qkv[:, :, :, 2 * head_dim :][rows]
    pair_lengths = jnp.sum(jnp.isfinite(pair_k[:, :, 0, 0]).astype(jnp.int32), axis=1)
    query_attn = attend_queries(query_qkv, head_dim)
    passage_attn = attend_pairs(query_qkv, pair_q, pair_k, pair_v, pair_lengths, head_dim, cands)
    return (query_attn, passage_attn)


def solution(mesh):
    in_specs = (
        P("store", None, "tp"),
        P("store", None, "tp"),
        P("store"),
        P("store"),
        P(),
        P(None, "tp", None),
    )
    out_specs = (P("store", None, "tp"), P("store", None, "tp"))
    return jax.shard_map(local, mesh=mesh, in_specs=in_specs, out_specs=out_specs, check_vma=False)
```

```python
import math

import jax
import jax.numpy as jnp
from jax import lax
from jax.sharding import PartitionSpec as P


def rms_rows(rows, norm_gain):
    values = rows.astype(jnp.float32)
    meansq = jnp.mean(values * values, axis=-1, keepdims=True)
    scaled = values * lax.rsqrt(meansq + 1e-05) * norm_gain.astype(jnp.float32)
    return scaled.astype(jnp.bfloat16)


def rotate_parts(raw, positions, head_dim):
    half_dim = head_dim // 2
    inverse = jnp.exp(
        jnp.arange(half_dim, dtype=jnp.float32) * (-2.0 * math.log(10000.0) / head_dim)
    )
    angles = positions[:, None] * inverse[None, :]
    cosine = jnp.cos(angles)[:, None, :]
    sine_part = jnp.sin(angles)[:, None, :]

    def turned(block):
        first = block[..., :half_dim]
        second = block[..., half_dim:]
        return jnp.concatenate(
            [first * cosine - second * sine_part, second * cosine + first * sine_part], axis=-1
        )

    queries = turned(raw[..., :head_dim])
    keyset = turned(raw[..., head_dim : 2 * head_dim])
    values = raw[..., 2 * head_dim :]
    return jnp.concatenate([queries, keyset, values], axis=-1).astype(jnp.bfloat16)


def softmax_rounded(scores, allowed):
    masked = jnp.where(allowed, scores, jnp.float32(-1e30))
    peak = jnp.max(masked, axis=-1, keepdims=True)
    expon = jnp.where(allowed, jnp.exp(masked - peak), jnp.float32(0.0))
    return (expon / jnp.sum(expon, axis=-1, keepdims=True)).astype(jnp.bfloat16)


def attend_queries(query_qkv, head_dim):
    count, query_len, heads = (query_qkv.shape[0], query_qkv.shape[1], query_qkv.shape[2])
    scale = head_dim ** (-0.5)
    scores = (
        jnp.einsum(
            "bqhd,bkhd->bhqk",
            query_qkv[..., :head_dim],
            query_qkv[..., head_dim : 2 * head_dim],
            preferred_element_type=jnp.float32,
        )
        * scale
    )
    steps_row = jnp.arange(query_len, dtype=jnp.int32)
    allowed = steps_row[:, None] >= steps_row[None, :]
    weights = softmax_rounded(scores, allowed[None, None])
    output = jnp.einsum(
        "bhqk,bkhd->bqhd",
        weights,
        query_qkv[..., 2 * head_dim :],
        preferred_element_type=jnp.float32,
    )
    return output.reshape(count, query_len, heads * head_dim).astype(jnp.bfloat16)


def attend_core(query_kv, pair_q, pair_k, pair_v, pair_lengths, head_dim):
    query_len = query_kv.shape[1]
    pairs, passage_len, heads = (pair_q.shape[0], pair_q.shape[1], pair_q.shape[2])
    scale = head_dim ** (-0.5)
    keyset = jnp.concatenate(
        [query_kv[..., :head_dim], pair_k], axis=1
    )
    values = jnp.concatenate([query_kv[..., head_dim:], pair_v], axis=1)
    scores = (
        jnp.einsum(
            "bihd,bthd->bhit", pair_q, keyset, preferred_element_type=jnp.float32
        )
        * scale
    )
    column = jnp.arange(query_len + passage_len, dtype=jnp.int32) - query_len
    row_index = jnp.arange(passage_len, dtype=jnp.int32)
    allowed = (column[None, None, :] < 0) | (column[None, None, :] <= row_index[None, :, None]) & (
        column[None, None, :] < pair_lengths[:, None, None]
    )
    weights = softmax_rounded(scores, allowed[:, None])
    output = jnp.einsum("bhit,bthd->bihd", weights, values, preferred_element_type=jnp.float32)
    live = row_index[None, :] < pair_lengths[:, None]
    output = jnp.where(live[:, :, None, None], output, jnp.float32(0.0))
    return output.reshape(pairs, passage_len, heads * head_dim).astype(jnp.bfloat16)


def attend_pairs(query_qkv, pair_q, pair_k, pair_v, pair_lengths, head_dim, cands):
    repeated = jnp.repeat(query_qkv[..., head_dim:], cands, axis=0)
    return attend_core(repeated, pair_q, pair_k, pair_v, pair_lengths, head_dim)


def gather_store(own):
    n_store = lax.axis_size("store")
    count = own.shape[0]
    if n_store > 8 or n_store % 2:
        return lax.all_gather(own, "store", axis=0, tiled=True), lambda rows: rows
    ring = [s for s in range(0, n_store, 2)] + [s for s in range(n_store - 1, 0, -2)]
    place = [0] * n_store
    for i, s in enumerate(ring):
        place[s] = i
    forward = [(ring[i], ring[(i + 1) % n_store]) for i in range(n_store)]
    backward = [(ring[(i + 1) % n_store], ring[i]) for i in range(n_store)]
    steps = []
    pieces = []
    for row in range(count):
        ahead_steps = n_store // 2 if row % 2 == 0 else (n_store - 1) // 2
        behind_steps = n_store - 1 - ahead_steps
        steps.append((ahead_steps, behind_steps))
        piece = own[row : row + 1]
        parts = [piece]
        ahead = piece
        behind = piece
        for k in range(max(ahead_steps, behind_steps)):
            if k < ahead_steps:
                ahead = lax.ppermute(ahead, "store", forward)
                parts.append(ahead)
            if k < behind_steps:
                behind = lax.ppermute(behind, "store", backward)
                parts.append(behind)
        pieces.append(parts)
    ordered = []
    arrival = []
    for row in range(count):
        ahead_steps, behind_steps = steps[row]
        parts = pieces[row]
        got_ahead, got_behind = [], []
        at = 1
        for k in range(max(ahead_steps, behind_steps)):
            if k < ahead_steps:
                got_ahead.append((parts[at], k + 1))
                at += 1
            if k < behind_steps:
                got_behind.append((parts[at], k + 1))
                at += 1
        for part, step in [(parts[0], 0)] + got_ahead + got_behind:
            ordered.append(part)
            arrival.append(step)
    def place_of(s):
        return jnp.where(s % 2 == 0, s // 2, n_store - 1 - s // 2)

    mine = place_of(lax.axis_index("store"))

    def rows_of(rows):
        dist = (place_of(rows // count) - mine) % n_store
        row = rows % count
        first = jnp.where(row % 2 == 0, n_store // 2, (n_store - 1) // 2)
        slot = jnp.where(dist == 0, 0, jnp.where(dist < n_store - first, first + dist, n_store - dist))
        return row * n_store + slot

    total = sum(part.shape[0] for part in ordered)
    row_at = lax.broadcasted_iota(jnp.int32, (total,) + own.shape[1:], 0)
    starts = []
    at = 0
    for part in ordered:
        starts.append(at)
        at += part.shape[0]

    def lay(joined, chosen):
        for part, at in chosen:
            size = part.shape[0]
            widened = jnp.pad(part, ((at, total - at - size),) + ((0, 0),) * (own.ndim - 1))
            if joined is None:
                joined = widened
            else:
                joined = jnp.where((row_at >= at) & (row_at < at + size), widened, joined)
        return joined

    last_step = max(arrival)
    first_join = min(1, last_step)
    joined = lay(None, [(p, a) for p, a, s in zip(ordered, starts, arrival) if s <= first_join])
    for step in range(first_join + 1, last_step + 1):
        joined = lax.optimization_barrier(joined)
        joined = lay(joined, [(p, a) for p, a, s in zip(ordered, starts, arrival) if s == step])
    return joined, rows_of


def local(query_embeds, passage_embeds, passage_lengths, cand_passage, norm_gain, w_qkv):
    quer_count, query_len, width_part = query_embeds.shape
    pass_count, passage_len = (passage_embeds.shape[0], passage_embeds.shape[1])
    pairs_dev = cand_passage.shape[0]
    cands = pairs_dev // quer_count
    heads_part = w_qkv.shape[1]
    head_dim = w_qkv.shape[2] // 3
    query_rows = query_embeds.reshape(quer_count * query_len, width_part)
    passage_rows = passage_embeds.reshape(pass_count * passage_len, width_part)
    query_pos = jnp.tile(jnp.arange(query_len, dtype=jnp.float32), quer_count)
    passage_pos = query_len + jnp.tile(jnp.arange(passage_len, dtype=jnp.float32), pass_count)
    query_total = quer_count * query_len
    all_rows = jnp.concatenate([query_rows, passage_rows], axis=0)
    full_rows = lax.all_gather(all_rows, "tp", axis=1, tiled=True)
    normed = rms_rows(full_rows, norm_gain)
    raw = jnp.einsum("nk,khc->nhc", normed, w_qkv, preferred_element_type=jnp.float32)
    projected = rotate_parts(raw, jnp.concatenate([query_pos, passage_pos], axis=0), head_dim)
    query_qkv = projected[:query_total].reshape(quer_count, query_len, heads_part, 3 * head_dim)
    own_qkv = projected[query_total:].reshape(pass_count, passage_len, heads_part, 3 * head_dim)
    padded = jnp.arange(passage_len, dtype=jnp.int32)[None, :] >= passage_lengths[:, None]
    head_at = lax.broadcasted_iota(jnp.int32, own_qkv.shape, 2)
    col_at = lax.broadcasted_iota(jnp.int32, own_qkv.shape, 3)
    mark = padded[:, :, None, None] & (head_at == 0) & (col_at == head_dim)
    own_qkv = jnp.where(mark, jnp.asarray(jnp.inf, own_qkv.dtype), own_qkv)
    store_qkv, rows_of = gather_store(own_qkv)
    rows = rows_of(cand_passage)
    pair_q = store_qkv[:, :, :, :head_dim][rows]
    pair_k = store_qkv[:, :, :, head_dim : 2 * head_dim][rows]
    pair_v = store_qkv[:, :, :, 2 * head_dim :][rows]
    pair_lengths = jnp.sum(jnp.isfinite(pair_k[:, :, 0, 0]).astype(jnp.int32), axis=1)
    query_attn = attend_queries(query_qkv, head_dim)
    passage_attn = attend_pairs(query_qkv, pair_q, pair_k, pair_v, pair_lengths, head_dim, cands)
    return (query_attn, passage_attn)


def solution(mesh):
    in_specs = (
        P("store", None, "tp"),
        P("store", None, "tp"),
        P("store"),
        P("store"),
        P(),
        P(None, "tp", None),
    )
    out_specs = (P("store", None, "tp"), P("store", None, "tp"))
    return jax.shard_map(local, mesh=mesh, in_specs=in_specs, out_specs=out_specs, check_vma=False)
```

```python
import math

import jax
import jax.numpy as jnp
from jax import lax
from jax.sharding import PartitionSpec as P


def rms_rows(rows, norm_gain):
    values = rows.astype(jnp.float32)
    meansq = jnp.mean(values * values, axis=-1, keepdims=True)
    scaled = values * lax.rsqrt(meansq + 1e-05) * norm_gain.astype(jnp.float32)
    return scaled.astype(jnp.bfloat16)


def rotate_parts(raw, positions, head_dim):
    half_dim = head_dim // 2
    inverse = jnp.exp(
        jnp.arange(half_dim, dtype=jnp.float32) * (-2.0 * math.log(10000.0) / head_dim)
    )
    angles = positions[:, None] * inverse[None, :]
    cosine = jnp.cos(angles)[:, None, :]
    sine_part = jnp.sin(angles)[:, None, :]

    def turned(block):
        first = block[..., :half_dim]
        second = block[..., half_dim:]
        return jnp.concatenate(
            [first * cosine - second * sine_part, second * cosine + first * sine_part], axis=-1
        )

    queries = turned(raw[..., :head_dim])
    keyset = turned(raw[..., head_dim : 2 * head_dim])
    values = raw[..., 2 * head_dim :]
    return jnp.concatenate([queries, keyset, values], axis=-1).astype(jnp.bfloat16)


def softmax_rounded(scores, allowed):
    masked = jnp.where(allowed, scores, jnp.float32(-1e30))
    peak = jnp.max(masked, axis=-1, keepdims=True)
    expon = jnp.where(allowed, jnp.exp(masked - peak), jnp.float32(0.0))
    return (expon / jnp.sum(expon, axis=-1, keepdims=True)).astype(jnp.bfloat16)


def attend_queries(query_qkv, head_dim):
    count, query_len, heads = (query_qkv.shape[0], query_qkv.shape[1], query_qkv.shape[2])
    scale = head_dim ** (-0.5)
    scores = (
        jnp.einsum(
            "bqhd,bkhd->bhqk",
            query_qkv[..., :head_dim],
            query_qkv[..., head_dim : 2 * head_dim],
            preferred_element_type=jnp.float32,
        )
        * scale
    )
    steps_row = jnp.arange(query_len, dtype=jnp.int32)
    allowed = steps_row[:, None] >= steps_row[None, :]
    weights = softmax_rounded(scores, allowed[None, None])
    output = jnp.einsum(
        "bhqk,bkhd->bqhd",
        weights,
        query_qkv[..., 2 * head_dim :],
        preferred_element_type=jnp.float32,
    )
    return output.reshape(count, query_len, heads * head_dim).astype(jnp.bfloat16)


def attend_core(query_kv, pair_q, pair_k, pair_v, pair_lengths, head_dim):
    query_len = query_kv.shape[1]
    pairs, passage_len, heads = (pair_q.shape[0], pair_q.shape[1], pair_q.shape[2])
    scale = head_dim ** (-0.5)
    to_query = jnp.einsum("bihd,bthd->bhit", pair_q, query_kv[..., :head_dim], preferred_element_type=jnp.float32) * scale
    to_own = jnp.einsum("bihd,bthd->bhit", pair_q, pair_k, preferred_element_type=jnp.float32) * scale
    row_index = jnp.arange(passage_len, dtype=jnp.int32)
    allowed = (row_index[None, None, :] <= row_index[None, :, None]) & (row_index[None, None, :] < pair_lengths[:, None, None])
    allowed = allowed[:, None]
    masked = jnp.where(allowed, to_own, jnp.float32(-1e30))
    peak = jnp.maximum(jnp.max(to_query, axis=-1, keepdims=True), jnp.max(masked, axis=-1, keepdims=True))
    exp_query = jnp.exp(to_query - peak)
    exp_own = jnp.where(allowed, jnp.exp(masked - peak), jnp.float32(0.0))
    total = jnp.sum(exp_query, axis=-1, keepdims=True) + jnp.sum(exp_own, axis=-1, keepdims=True)
    weight_query = (exp_query / total).astype(jnp.bfloat16)
    weight_own = (exp_own / total).astype(jnp.bfloat16)
    output = jnp.einsum("bhit,bthd->bihd", weight_query, query_kv[..., head_dim:], preferred_element_type=jnp.float32) + jnp.einsum(
        "bhit,bthd->bihd", weight_own, pair_v, preferred_element_type=jnp.float32
    )
    live = row_index[None, :] < pair_lengths[:, None]
    output = jnp.where(live[:, :, None, None], output, jnp.float32(0.0))
    return output.reshape(pairs, passage_len, heads * head_dim).astype(jnp.bfloat16)


def attend_pairs(query_qkv, pair_q, pair_k, pair_v, pair_lengths, head_dim, cands):
    repeated = jnp.repeat(query_qkv[..., head_dim:], cands, axis=0)
    return attend_core(repeated, pair_q, pair_k, pair_v, pair_lengths, head_dim)


def gather_store(own):
    n_store = lax.axis_size("store")
    count = own.shape[0]
    if n_store > 8 or n_store % 2:
        return lax.all_gather(own, "store", axis=0, tiled=True), lambda rows: rows
    ring = [s for s in range(0, n_store, 2)] + [s for s in range(n_store - 1, 0, -2)]
    place = [0] * n_store
    for i, s in enumerate(ring):
        place[s] = i
    forward = [(ring[i], ring[(i + 1) % n_store]) for i in range(n_store)]
    backward = [(ring[(i + 1) % n_store], ring[i]) for i in range(n_store)]
    steps = []
    pieces = []
    for row in range(count):
        ahead_steps = n_store // 2 if row % 2 == 0 else (n_store - 1) // 2
        behind_steps = n_store - 1 - ahead_steps
        steps.append((ahead_steps, behind_steps))
        piece = own[row : row + 1]
        parts = [piece]
        ahead = piece
        behind = piece
        for k in range(max(ahead_steps, behind_steps)):
            if k < ahead_steps:
                ahead = lax.ppermute(ahead, "store", forward)
                parts.append(ahead)
            if k < behind_steps:
                behind = lax.ppermute(behind, "store", backward)
                parts.append(behind)
        pieces.append(parts)
    ordered = []
    arrival = []
    for row in range(count):
        ahead_steps, behind_steps = steps[row]
        parts = pieces[row]
        got_ahead, got_behind = [], []
        at = 1
        for k in range(max(ahead_steps, behind_steps)):
            if k < ahead_steps:
                got_ahead.append((parts[at], k + 1))
                at += 1
            if k < behind_steps:
                got_behind.append((parts[at], k + 1))
                at += 1
        for part, step in [(parts[0], 0)] + got_ahead + got_behind:
            ordered.append(part)
            arrival.append(step)
    def place_of(s):
        return jnp.where(s % 2 == 0, s // 2, n_store - 1 - s // 2)

    mine = place_of(lax.axis_index("store"))

    def rows_of(rows):
        dist = (place_of(rows // count) - mine) % n_store
        row = rows % count
        first = jnp.where(row % 2 == 0, n_store // 2, (n_store - 1) // 2)
        slot = jnp.where(dist == 0, 0, jnp.where(dist < n_store - first, first + dist, n_store - dist))
        return row * n_store + slot

    total = sum(part.shape[0] for part in ordered)
    row_at = lax.broadcasted_iota(jnp.int32, (total,) + own.shape[1:], 0)
    starts = []
    at = 0
    for part in ordered:
        starts.append(at)
        at += part.shape[0]

    def lay(joined, chosen):
        for part, at in chosen:
            size = part.shape[0]
            widened = jnp.pad(part, ((at, total - at - size),) + ((0, 0),) * (own.ndim - 1))
            if joined is None:
                joined = widened
            else:
                joined = jnp.where((row_at >= at) & (row_at < at + size), widened, joined)
        return joined

    last_step = max(arrival)
    first_join = min(1, last_step)
    joined = lay(None, [(p, a) for p, a, s in zip(ordered, starts, arrival) if s <= first_join])
    for step in range(first_join + 1, last_step + 1):
        joined = lax.optimization_barrier(joined)
        joined = lay(joined, [(p, a) for p, a, s in zip(ordered, starts, arrival) if s == step])
    return joined, rows_of


def local(query_embeds, passage_embeds, passage_lengths, cand_passage, norm_gain, w_qkv):
    quer_count, query_len, width_part = query_embeds.shape
    pass_count, passage_len = (passage_embeds.shape[0], passage_embeds.shape[1])
    pairs_dev = cand_passage.shape[0]
    cands = pairs_dev // quer_count
    heads_part = w_qkv.shape[1]
    head_dim = w_qkv.shape[2] // 3
    query_rows = query_embeds.reshape(quer_count * query_len, width_part)
    passage_rows = passage_embeds.reshape(pass_count * passage_len, width_part)
    query_pos = jnp.tile(jnp.arange(query_len, dtype=jnp.float32), quer_count)
    passage_pos = query_len + jnp.tile(jnp.arange(passage_len, dtype=jnp.float32), pass_count)
    query_total = quer_count * query_len
    all_rows = jnp.concatenate([query_rows, passage_rows], axis=0)
    full_rows = lax.all_gather(all_rows, "tp", axis=1, tiled=True)
    normed = rms_rows(full_rows, norm_gain)
    raw = jnp.einsum("nk,khc->nhc", normed, w_qkv, preferred_element_type=jnp.float32)
    projected = rotate_parts(raw, jnp.concatenate([query_pos, passage_pos], axis=0), head_dim)
    query_qkv = projected[:query_total].reshape(quer_count, query_len, heads_part, 3 * head_dim)
    own_qkv = projected[query_total:].reshape(pass_count, passage_len, heads_part, 3 * head_dim)
    padded = jnp.arange(passage_len, dtype=jnp.int32)[None, :] >= passage_lengths[:, None]
    head_at = lax.broadcasted_iota(jnp.int32, own_qkv.shape, 2)
    col_at = lax.broadcasted_iota(jnp.int32, own_qkv.shape, 3)
    mark = padded[:, :, None, None] & (head_at == 0) & (col_at == head_dim)
    own_qkv = jnp.where(mark, jnp.asarray(jnp.inf, own_qkv.dtype), own_qkv)
    store_qkv, rows_of = gather_store(own_qkv)
    rows = rows_of(cand_passage)
    pair_q = store_qkv[:, :, :, :head_dim][rows]
    pair_k = store_qkv[:, :, :, head_dim : 2 * head_dim][rows]
    pair_v = store_qkv[:, :, :, 2 * head_dim :][rows]
    pair_lengths = jnp.sum(jnp.isfinite(pair_k[:, :, 0, 0]).astype(jnp.int32), axis=1)
    query_attn = attend_queries(query_qkv, head_dim)
    passage_attn = attend_pairs(query_qkv, pair_q, pair_k, pair_v, pair_lengths, head_dim, cands)
    return (query_attn, passage_attn)


def solution(mesh):
    in_specs = (
        P("store", None, "tp"),
        P("store", None, "tp"),
        P("store"),
        P("store"),
        P(),
        P(None, "tp", None),
    )
    out_specs = (P("store", None, "tp"), P("store", None, "tp"))
    return jax.shard_map(local, mesh=mesh, in_specs=in_specs, out_specs=out_specs, check_vma=False)
```

```python
import math

import jax
import jax.numpy as jnp
from jax import lax
from jax.sharding import PartitionSpec as P


def rms_rows(rows, norm_gain):
    values = rows.astype(jnp.float32)
    meansq = jnp.mean(values * values, axis=-1, keepdims=True)
    scaled = values * lax.rsqrt(meansq + 1e-05) * norm_gain.astype(jnp.float32)
    return scaled.astype(jnp.bfloat16)


def rotate_parts(raw, positions, head_dim):
    half_dim = head_dim // 2
    inverse = jnp.exp(
        jnp.arange(half_dim, dtype=jnp.float32) * (-2.0 * math.log(10000.0) / head_dim)
    )
    angles = positions[:, None] * inverse[None, :]
    cosine = jnp.cos(angles)[:, None, :]
    sine_part = jnp.sin(angles)[:, None, :]

    def turned(block):
        first = block[..., :half_dim]
        second = block[..., half_dim:]
        return jnp.concatenate(
            [first * cosine - second * sine_part, second * cosine + first * sine_part], axis=-1
        )

    queries = turned(raw[..., :head_dim])
    keyset = turned(raw[..., head_dim : 2 * head_dim])
    values = raw[..., 2 * head_dim :]
    return jnp.concatenate([queries, keyset, values], axis=-1).astype(jnp.bfloat16)


def softmax_rounded(scores, allowed):
    masked = jnp.where(allowed, scores, jnp.float32(-1e30))
    peak = jnp.max(masked, axis=-1, keepdims=True)
    expon = jnp.where(allowed, jnp.exp(masked - peak), jnp.float32(0.0))
    return (expon / jnp.sum(expon, axis=-1, keepdims=True)).astype(jnp.bfloat16)


def attend_queries(query_qkv, head_dim):
    count, query_len, heads = (query_qkv.shape[0], query_qkv.shape[1], query_qkv.shape[2])
    scale = head_dim ** (-0.5)
    scores = (
        jnp.einsum(
            "bqhd,bkhd->bhqk",
            query_qkv[..., :head_dim],
            query_qkv[..., head_dim : 2 * head_dim],
            preferred_element_type=jnp.float32,
        )
        * scale
    )
    steps_row = jnp.arange(query_len, dtype=jnp.int32)
    allowed = steps_row[:, None] >= steps_row[None, :]
    weights = softmax_rounded(scores, allowed[None, None])
    output = jnp.einsum(
        "bhqk,bkhd->bqhd",
        weights,
        query_qkv[..., 2 * head_dim :],
        preferred_element_type=jnp.float32,
    )
    return output.reshape(count, query_len, heads * head_dim).astype(jnp.bfloat16)


def attend_core(query_kv, pair_q, pair_k, pair_v, pair_lengths, head_dim):
    query_len = query_kv.shape[1]
    pairs, passage_len, heads = (pair_q.shape[0], pair_q.shape[1], pair_q.shape[2])
    scale = head_dim ** (-0.5)
    keyset = jnp.concatenate(
        [query_kv[..., :head_dim], pair_k], axis=1
    )
    values = jnp.concatenate([query_kv[..., head_dim:], pair_v], axis=1)
    scores = (
        jnp.einsum(
            "bihd,bthd->bhit", pair_q, keyset, preferred_element_type=jnp.float32
        )
        * scale
    )
    column = jnp.arange(query_len + passage_len, dtype=jnp.int32) - query_len
    row_index = jnp.arange(passage_len, dtype=jnp.int32)
    allowed = (column[None, None, :] < 0) | (column[None, None, :] <= row_index[None, :, None]) & (
        column[None, None, :] < pair_lengths[:, None, None]
    )
    weights = softmax_rounded(scores, allowed[:, None])
    output = jnp.einsum("bhit,bthd->bihd", weights, values, preferred_element_type=jnp.float32)
    live = row_index[None, :] < pair_lengths[:, None]
    output = jnp.where(live[:, :, None, None], output, jnp.float32(0.0))
    return output.reshape(pairs, passage_len, heads * head_dim).astype(jnp.bfloat16)


def attend_pairs(query_qkv, pair_q, pair_k, pair_v, pair_lengths, head_dim, cands):
    repeated = jnp.repeat(query_qkv[..., head_dim:], cands, axis=0)
    return attend_core(repeated, pair_q, pair_k, pair_v, pair_lengths, head_dim)


def gather_store(own):
    n_store = lax.axis_size("store")
    count = own.shape[0]
    if n_store > 8 or n_store % 2:
        return lax.all_gather(own, "store", axis=0, tiled=True), lambda rows: rows
    ring = [s for s in range(0, n_store, 2)] + [s for s in range(n_store - 1, 0, -2)]
    place = [0] * n_store
    for i, s in enumerate(ring):
        place[s] = i
    forward = [(ring[i], ring[(i + 1) % n_store]) for i in range(n_store)]
    backward = [(ring[(i + 1) % n_store], ring[i]) for i in range(n_store)]
    half = n_store // 2
    if count == 2:
        ordered = [own]
        arrival = [0]
        ahead_parts, behind_parts = [], []
        ahead = own
        behind = own
        for k in range(1, half):
            ahead = lax.ppermute(ahead, "store", forward)
            behind = lax.ppermute(behind, "store", backward)
            ahead_parts.append((ahead, k))
            behind_parts.append((behind, k))
        ahead_parts.append((lax.ppermute(ahead[0:1], "store", forward), half))
        behind_parts.append((lax.ppermute(behind[1:2], "store", backward), half))
        for part, step in ahead_parts[:-1] + behind_parts[:-1] + [ahead_parts[-1], behind_parts[-1]]:
            ordered.append(part)
            arrival.append(step)
    else:
        steps = []
        pieces = []
        for row in range(count):
            ahead_steps = n_store // 2 if row % 2 == 0 else (n_store - 1) // 2
            behind_steps = n_store - 1 - ahead_steps
            steps.append((ahead_steps, behind_steps))
            piece = own[row : row + 1]
            parts = [piece]
            ahead = piece
            behind = piece
            for k in range(max(ahead_steps, behind_steps)):
                if k < ahead_steps:
                    ahead = lax.ppermute(ahead, "store", forward)
                    parts.append(ahead)
                if k < behind_steps:
                    behind = lax.ppermute(behind, "store", backward)
                    parts.append(behind)
            pieces.append(parts)
        ordered = []
        arrival = []
        for row in range(count):
            ahead_steps, behind_steps = steps[row]
            parts = pieces[row]
            got_ahead, got_behind = [], []
            at = 1
            for k in range(max(ahead_steps, behind_steps)):
                if k < ahead_steps:
                    got_ahead.append((parts[at], k + 1))
                    at += 1
                if k < behind_steps:
                    got_behind.append((parts[at], k + 1))
                    at += 1
            for part, step in [(parts[0], 0)] + got_ahead + got_behind:
                ordered.append(part)
                arrival.append(step)
    def place_of(s):
        return jnp.where(s % 2 == 0, s // 2, n_store - 1 - s // 2)

    mine = place_of(lax.axis_index("store"))

    def rows_of(rows):
        dist = (place_of(rows // count) - mine) % n_store
        row = rows % count
        if count == 2:
            far = jnp.where(dist > half, 2 * (n_store - dist), 2 * half + 2 * (dist - 1))
            return jnp.where(dist == 0, row, jnp.where(dist == half, 4 * half - 2, far) + row)
        first = jnp.where(row % 2 == 0, n_store // 2, (n_store - 1) // 2)
        slot = jnp.where(dist == 0, 0, jnp.where(dist < n_store - first, first + dist, n_store - dist))
        return row * n_store + slot

    total = sum(part.shape[0] for part in ordered)
    row_at = lax.broadcasted_iota(jnp.int32, (total,) + own.shape[1:], 0)
    starts = []
    at = 0
    for part in ordered:
        starts.append(at)
        at += part.shape[0]

    def lay(joined, chosen):
        for part, at in chosen:
            size = part.shape[0]
            widened = jnp.pad(part, ((at, total - at - size),) + ((0, 0),) * (own.ndim - 1))
            if joined is None:
                joined = widened
            else:
                joined = jnp.where((row_at >= at) & (row_at < at + size), widened, joined)
        return joined

    last_step = max(arrival)
    first_join = min(1, last_step)
    joined = lay(None, [(p, a) for p, a, s in zip(ordered, starts, arrival) if s <= first_join])
    for step in range(first_join + 1, last_step + 1):
        joined = lax.optimization_barrier(joined)
        joined = lay(joined, [(p, a) for p, a, s in zip(ordered, starts, arrival) if s == step])
    return joined, rows_of


def local(query_embeds, passage_embeds, passage_lengths, cand_passage, norm_gain, w_qkv):
    quer_count, query_len, width_part = query_embeds.shape
    pass_count, passage_len = (passage_embeds.shape[0], passage_embeds.shape[1])
    pairs_dev = cand_passage.shape[0]
    cands = pairs_dev // quer_count
    heads_part = w_qkv.shape[1]
    head_dim = w_qkv.shape[2] // 3
    query_rows = query_embeds.reshape(quer_count * query_len, width_part)
    passage_rows = passage_embeds.reshape(pass_count * passage_len, width_part)
    query_pos = jnp.tile(jnp.arange(query_len, dtype=jnp.float32), quer_count)
    passage_pos = query_len + jnp.tile(jnp.arange(passage_len, dtype=jnp.float32), pass_count)
    query_total = quer_count * query_len
    all_rows = jnp.concatenate([query_rows, passage_rows], axis=0)
    full_rows = lax.all_gather(all_rows, "tp", axis=1, tiled=True)
    normed = rms_rows(full_rows, norm_gain)
    raw = jnp.einsum("nk,khc->nhc", normed, w_qkv, preferred_element_type=jnp.float32)
    projected = rotate_parts(raw, jnp.concatenate([query_pos, passage_pos], axis=0), head_dim)
    query_qkv = projected[:query_total].reshape(quer_count, query_len, heads_part, 3 * head_dim)
    own_qkv = projected[query_total:].reshape(pass_count, passage_len, heads_part, 3 * head_dim)
    padded = jnp.arange(passage_len, dtype=jnp.int32)[None, :] >= passage_lengths[:, None]
    head_at = lax.broadcasted_iota(jnp.int32, own_qkv.shape, 2)
    col_at = lax.broadcasted_iota(jnp.int32, own_qkv.shape, 3)
    mark = padded[:, :, None, None] & (head_at == 0) & (col_at == head_dim)
    own_qkv = jnp.where(mark, jnp.asarray(jnp.inf, own_qkv.dtype), own_qkv)
    store_qkv, rows_of = gather_store(own_qkv)
    rows = rows_of(cand_passage)
    pair_q = store_qkv[:, :, :, :head_dim][rows]
    pair_k = store_qkv[:, :, :, head_dim : 2 * head_dim][rows]
    pair_v = store_qkv[:, :, :, 2 * head_dim :][rows]
    pair_lengths = jnp.sum(jnp.isfinite(pair_k[:, :, 0, 0]).astype(jnp.int32), axis=1)
    query_attn = attend_queries(query_qkv, head_dim)
    passage_attn = attend_pairs(query_qkv, pair_q, pair_k, pair_v, pair_lengths, head_dim, cands)
    return (query_attn, passage_attn)


def solution(mesh):
    in_specs = (
        P("store", None, "tp"),
        P("store", None, "tp"),
        P("store"),
        P("store"),
        P(),
        P(None, "tp", None),
    )
    out_specs = (P("store", None, "tp"), P("store", None, "tp"))
    return jax.shard_map(local, mesh=mesh, in_specs=in_specs, out_specs=out_specs, check_vma=False)
```

```python
import math

import jax
import jax.numpy as jnp
from jax import lax
from jax.sharding import PartitionSpec as P


def rms_rows(rows, norm_gain):
    values = rows.astype(jnp.float32)
    meansq = jnp.mean(values * values, axis=-1, keepdims=True)
    scaled = values * lax.rsqrt(meansq + 1e-05) * norm_gain.astype(jnp.float32)
    return scaled.astype(jnp.bfloat16)


def rotate_parts(raw, positions, head_dim):
    half_dim = head_dim // 2
    inverse = jnp.exp(
        jnp.arange(half_dim, dtype=jnp.float32) * (-2.0 * math.log(10000.0) / head_dim)
    )
    angles = positions[:, None] * inverse[None, :]
    cosine = jnp.cos(angles)[:, None, :]
    sine_part = jnp.sin(angles)[:, None, :]

    def turned(block):
        first = block[..., :half_dim]
        second = block[..., half_dim:]
        return jnp.concatenate(
            [first * cosine - second * sine_part, second * cosine + first * sine_part], axis=-1
        )

    queries = turned(raw[..., :head_dim])
    keyset = turned(raw[..., head_dim : 2 * head_dim])
    values = raw[..., 2 * head_dim :]
    return jnp.concatenate([queries, keyset, values], axis=-1).astype(jnp.bfloat16)


def softmax_rounded(scores, allowed):
    masked = jnp.where(allowed, scores, jnp.float32(-1e30))
    peak = jnp.max(masked, axis=-1, keepdims=True)
    expon = jnp.where(allowed, jnp.exp(masked - peak), jnp.float32(0.0))
    return (expon / jnp.sum(expon, axis=-1, keepdims=True)).astype(jnp.bfloat16)


def attend_queries(query_qkv, head_dim):
    count, query_len, heads = (query_qkv.shape[0], query_qkv.shape[1], query_qkv.shape[2])
    scale = head_dim ** (-0.5)
    scores = (
        jnp.einsum(
            "bqhd,bkhd->bhqk",
            query_qkv[..., :head_dim],
            query_qkv[..., head_dim : 2 * head_dim],
            preferred_element_type=jnp.float32,
        )
        * scale
    )
    steps_row = jnp.arange(query_len, dtype=jnp.int32)
    allowed = steps_row[:, None] >= steps_row[None, :]
    weights = softmax_rounded(scores, allowed[None, None])
    output = jnp.einsum(
        "bhqk,bkhd->bqhd",
        weights,
        query_qkv[..., 2 * head_dim :],
        preferred_element_type=jnp.float32,
    )
    return output.reshape(count, query_len, heads * head_dim).astype(jnp.bfloat16)


def attend_core(query_kv, pair_q, pair_k, pair_v, pair_lengths, head_dim):
    query_len = query_kv.shape[1]
    pairs, passage_len, heads = (pair_q.shape[0], pair_q.shape[1], pair_q.shape[2])
    scale = head_dim ** (-0.5)
    keyset = jnp.concatenate(
        [query_kv[..., :head_dim], pair_k], axis=1
    )
    values = jnp.concatenate([query_kv[..., head_dim:], pair_v], axis=1)
    scores = (
        jnp.einsum(
            "bihd,bthd->bhit", pair_q, keyset, preferred_element_type=jnp.float32
        )
        * scale
    )
    column = jnp.arange(query_len + passage_len, dtype=jnp.int32) - query_len
    row_index = jnp.arange(passage_len, dtype=jnp.int32)
    allowed = (column[None, None, :] < 0) | (column[None, None, :] <= row_index[None, :, None]) & (
        column[None, None, :] < pair_lengths[:, None, None]
    )
    weights = softmax_rounded(scores, allowed[:, None])
    output = jnp.einsum("bhit,bthd->bihd", weights, values, preferred_element_type=jnp.float32)
    live = row_index[None, :] < pair_lengths[:, None]
    output = jnp.where(live[:, :, None, None], output, jnp.float32(0.0))
    return output.reshape(pairs, passage_len, heads * head_dim).astype(jnp.bfloat16)


def attend_pairs(query_qkv, pair_q, pair_k, pair_v, pair_lengths, head_dim, cands):
    repeated = jnp.repeat(query_qkv[..., head_dim:], cands, axis=0)
    return attend_core(repeated, pair_q, pair_k, pair_v, pair_lengths, head_dim)


def gather_store(own):
    n_store = lax.axis_size("store")
    count = own.shape[0]
    if n_store > 8 or n_store % 2:
        return lax.all_gather(own, "store", axis=0, tiled=True), lambda rows: rows
    ring = [s for s in range(0, n_store, 2)] + [s for s in range(n_store - 1, 0, -2)]
    place = [0] * n_store
    for i, s in enumerate(ring):
        place[s] = i
    forward = [(ring[i], ring[(i + 1) % n_store]) for i in range(n_store)]
    backward = [(ring[(i + 1) % n_store], ring[i]) for i in range(n_store)]
    steps = []
    pieces = []
    for row in range(count):
        ahead_steps = n_store // 2 if row % 2 == 0 else (n_store - 1) // 2
        behind_steps = n_store - 1 - ahead_steps
        steps.append((ahead_steps, behind_steps))
        piece = own[row : row + 1]
        parts = [piece]
        ahead = piece
        behind = piece
        for k in range(max(ahead_steps, behind_steps)):
            if k < ahead_steps:
                ahead = lax.ppermute(ahead, "store", forward)
                parts.append(ahead)
            if k < behind_steps:
                behind = lax.ppermute(behind, "store", backward)
                parts.append(behind)
        pieces.append(parts)
    ordered = []
    arrival = []
    for row in range(count):
        ahead_steps, behind_steps = steps[row]
        parts = pieces[row]
        got_ahead, got_behind = [], []
        at = 1
        for k in range(max(ahead_steps, behind_steps)):
            if k < ahead_steps:
                got_ahead.append((parts[at], k + 1))
                at += 1
            if k < behind_steps:
                got_behind.append((parts[at], k + 1))
                at += 1
        for part, step in [(parts[0], 0)] + got_ahead + got_behind:
            ordered.append(part)
            arrival.append(step)
    def place_of(s):
        return jnp.where(s % 2 == 0, s // 2, n_store - 1 - s // 2)

    mine = place_of(lax.axis_index("store"))

    def rows_of(rows):
        dist = (place_of(rows // count) - mine) % n_store
        row = rows % count
        first = jnp.where(row % 2 == 0, n_store // 2, (n_store - 1) // 2)
        slot = jnp.where(dist == 0, 0, jnp.where(dist < n_store - first, first + dist, n_store - dist))
        return row * n_store + slot

    total = sum(part.shape[0] for part in ordered)
    row_at = lax.broadcasted_iota(jnp.int32, (total,) + own.shape[1:], 0)
    starts = []
    at = 0
    for part in ordered:
        starts.append(at)
        at += part.shape[0]

    def lay(joined, chosen):
        for part, at in chosen:
            size = part.shape[0]
            widened = jnp.pad(part, ((at, total - at - size),) + ((0, 0),) * (own.ndim - 1))
            if joined is None:
                joined = widened
            else:
                joined = jnp.where((row_at >= at) & (row_at < at + size), widened, joined)
        return joined

    last_step = max(arrival)
    first_join = min(1, last_step)
    joined = lay(None, [(p, a) for p, a, s in zip(ordered, starts, arrival) if s <= first_join])
    for step in range(first_join + 1, last_step + 1):
        joined = lax.optimization_barrier(joined)
        joined = lay(joined, [(p, a) for p, a, s in zip(ordered, starts, arrival) if s == step])
    return joined, rows_of


def local(query_embeds, passage_embeds, passage_lengths, cand_passage, norm_gain, w_qkv):
    quer_count, query_len, width_part = query_embeds.shape
    pass_count, passage_len = (passage_embeds.shape[0], passage_embeds.shape[1])
    pairs_dev = cand_passage.shape[0]
    cands = pairs_dev // quer_count
    heads_part = w_qkv.shape[1]
    head_dim = w_qkv.shape[2] // 3
    query_rows = query_embeds.reshape(quer_count * query_len, width_part)
    passage_rows = passage_embeds.reshape(pass_count * passage_len, width_part)
    query_pos = jnp.tile(jnp.arange(query_len, dtype=jnp.float32), quer_count)
    passage_pos = query_len + jnp.tile(jnp.arange(passage_len, dtype=jnp.float32), pass_count)
    query_total = quer_count * query_len
    all_rows = jnp.concatenate([query_rows, passage_rows], axis=0)
    n_tp = lax.axis_size("tp")
    blocks = lax.all_gather(all_rows, "tp", axis=0, tiled=False).astype(jnp.float32)
    meansq = jnp.mean(blocks * blocks, axis=(0, 2))
    gain = norm_gain.astype(jnp.float32).reshape(n_tp, 1, width_part)
    normed = (blocks * lax.rsqrt(meansq + 1e-05)[None, :, None] * gain).astype(jnp.bfloat16)
    w_blocks = w_qkv.reshape(n_tp, width_part, heads_part, 3 * head_dim)
    raw = jnp.einsum("tnk,tkhc->nhc", normed, w_blocks, preferred_element_type=jnp.float32)
    projected = rotate_parts(raw, jnp.concatenate([query_pos, passage_pos], axis=0), head_dim)
    query_qkv = projected[:query_total].reshape(quer_count, query_len, heads_part, 3 * head_dim)
    own_qkv = projected[query_total:].reshape(pass_count, passage_len, heads_part, 3 * head_dim)
    padded = jnp.arange(passage_len, dtype=jnp.int32)[None, :] >= passage_lengths[:, None]
    head_at = lax.broadcasted_iota(jnp.int32, own_qkv.shape, 2)
    col_at = lax.broadcasted_iota(jnp.int32, own_qkv.shape, 3)
    mark = padded[:, :, None, None] & (head_at == 0) & (col_at == head_dim)
    own_qkv = jnp.where(mark, jnp.asarray(jnp.inf, own_qkv.dtype), own_qkv)
    store_qkv, rows_of = gather_store(own_qkv)
    rows = rows_of(cand_passage)
    pair_q = store_qkv[:, :, :, :head_dim][rows]
    pair_k = store_qkv[:, :, :, head_dim : 2 * head_dim][rows]
    pair_v = store_qkv[:, :, :, 2 * head_dim :][rows]
    pair_lengths = jnp.sum(jnp.isfinite(pair_k[:, :, 0, 0]).astype(jnp.int32), axis=1)
    query_attn = attend_queries(query_qkv, head_dim)
    passage_attn = attend_pairs(query_qkv, pair_q, pair_k, pair_v, pair_lengths, head_dim, cands)
    return (query_attn, passage_attn)


def solution(mesh):
    in_specs = (
        P("store", None, "tp"),
        P("store", None, "tp"),
        P("store"),
        P("store"),
        P(),
        P(None, "tp", None),
    )
    out_specs = (P("store", None, "tp"), P("store", None, "tp"))
    return jax.shard_map(local, mesh=mesh, in_specs=in_specs, out_specs=out_specs, check_vma=False)
```
